32 devices in a mesh: species: 4 (over z), space: 8 (over y, x, core).
Axes of the slice: x: 2, y: 2, z: 4, core: 2. Of those that a mesh axis runs over, the one named last changes fastest.
Arguments:
- density: float32 [4, 32, 16, 32, 128], P('species', None, 'space'), may hold values from 0 to 2
- space_factor: float32 [16, 32, 128], P('space'), may hold values from 0.5 to 1
- diff_rate: float32 [4, 32], P('species'), may hold values from 0.02 to 0.08
- loss_inverse: float32 [4, 32, 32], P('species'), may hold values from 0 to 1, as said below
- chain_yield: float32 [4, 32], P('species'), may hold values from 0.25 to 0.95
- survival: float32 [4, 32], P('species'), may hold values from 0.6 to 1
- gamma_yield: float32 [4, 32], P('species'), may hold values from 0.1 to 1
- sky_weight: bfloat16 [8, 8, 64, 128], P('space'), may hold values from -0.75 to 0.75
- sky_blocks: int32 [8, 8], P('space'), may hold values from 0 to 383
Outputs:
- propagated: float32 [4, 32, 16, 32, 128], P('species', None, 'space')
- sky: float32 [384, 128], P('space')
The draws below stay inside these ranges and needn't reach their ends.
Inputs may be any that keep to these rules, and one draw needn't show every extreme that they name: `loss_inverse`: each matrix is upper triangular with a diagonal of 0.5 to 1 and nonnegative entries.
All inputs are finite; a program needn't handle non-finite values.
Results may differ from the reference program's by a relative error of at most 0.0011.
Values sent between devices are 32-bit elements; how exact they have to be, the bound alone decides.
No kernel may reach another device: no remote copies, remote signals or barrier semaphores. Data moves between devices by JAX's collectives and lax.ppermute only.
A program may use at most 64 MiB of HBM per device.

```python
import math
import jax
import jax.numpy as jnp
from jax import lax

P_SIZE = 32
CX = 2
NY = 32
NZ = 128
SUBSTEPS = 2
PB = 128
NL = 8
NB = 384
NG = 4
TILES = 8
NX = 16


def draw_loss_inverse(key, part):
    first, second = jax.random.split(key)
    diagonal = jax.random.uniform(first, (NG, P_SIZE), jnp.float32, 0.5, 1.0)
    upper = jax.random.uniform(second, (NG, P_SIZE, P_SIZE), jnp.float32, 0.0, 2.0) / P_SIZE
    rows = jnp.arange(P_SIZE)[:, None]
    cols = jnp.arange(P_SIZE)[None, :]
    strict = (cols > rows).astype(jnp.float32)
    ident = (cols == rows).astype(jnp.float32)
    return upper * strict[None] + diagonal[:, :, None] * ident[None]


def plant(array, rng, low, high):
    longest = array.shape.index(max(array.shape))
    spots = []
    for shift in (0, 1):
        where = [jax.random.randint(jax.random.fold_in(rng, axis), (), 0, length) for axis, length in enumerate(array.shape)]
        where[longest] = (where[longest] + shift) % array.shape[longest]
        spots.append(tuple(where))
    return array.at[spots[0]].set(low).at[spots[1]].set(high)


def level_of(stream_key, dims, cuts, low, largest):
    loudness, own = 1.0, jax.random.fold_in(stream_key, 6)
    for dim, shards_of in cuts:
        draws = jnp.exp(jax.random.uniform(jax.random.fold_in(own, dim), (shards_of,), jnp.float32, low / len(cuts), largest / len(cuts)))
        loudness = loudness * jnp.repeat(draws, dims[dim] // shards_of).reshape([-1 if axis == dim else 1 for axis in range(len(dims))])
    return loudness


def centred(stream_key, extent, spread, limit, shards=(), kind=jnp.bfloat16):
    values = jax.random.normal(stream_key, extent, jnp.float32) * spread
    if len(shards) > 0:
        values = level_of(stream_key, extent, shards, -0.22, 0.18) * values
    return jnp.clip(values, min=-limit, max=limit).astype(kind)


def setup_inputs(seed: int = 0) -> dict:
    key_list = jax.random.split(jax.random.key(seed), 10)
    density = jnp.clip(2.0 * jax.random.uniform(key_list[0], (NG, P_SIZE, NX, NY, NZ), jnp.float32) ** level_of(key_list[0], (NG, P_SIZE, NX, NY, NZ), ((0, 4), (2, 8)), -0.2, 0.2), 0.0, 2.0)
    space_factor = jnp.clip(0.5 + 0.5 * jax.random.uniform(key_list[1], (NX, NY, NZ), jnp.float32) ** level_of(key_list[1], (NX, NY, NZ), ((0, 8),), -0.2, 0.2), 0.5, 1.0)
    diff_rate = jnp.clip(jnp.exp(math.log(0.08) - 1.3862944 * jax.random.uniform(key_list[2], (NG, P_SIZE), jnp.float32) ** level_of(key_list[2], (NG, P_SIZE), ((0, 4),), -0.2, 0.2)), 0.02, 0.08)
    loss_inverse = draw_loss_inverse(jax.random.fold_in(key_list[9], 71), 0)
    chain_yield = jnp.clip(jnp.exp(math.log(0.95) - 1.3350011 * jax.random.uniform(key_list[4], (NG, P_SIZE), jnp.float32) ** level_of(key_list[4], (NG, P_SIZE), ((0, 4),), -0.2, 0.2)), 0.25, 0.95)
    survival = jnp.clip(0.6 + 0.39999998 * jax.random.uniform(key_list[5], (NG, P_SIZE), jnp.float32) ** level_of(key_list[5], (NG, P_SIZE), ((0, 4),), -0.2, 0.2), 0.6, 1.0)
    gamma_yield = jnp.clip(jnp.exp(math.log(1.0) - 2.3025851 * jax.random.uniform(key_list[6], (NG, P_SIZE), jnp.float32) ** level_of(key_list[6], (NG, P_SIZE), ((0, 4),), -0.2, 0.2)), 0.1, 1.0)
    sky_weight = centred(key_list[7], (TILES, NL, CX * NY, PB), (CX * NY) ** -0.5, 0.75, ((0, 8),))
    sky_blocks = plant(jax.random.randint(key_list[8], (TILES, NL), 0, NB), jax.random.fold_in(key_list[8], 1), 0, NB - 1).astype(jnp.int32)
    return dict(density=density, space_factor=space_factor, diff_rate=diff_rate, loss_inverse=loss_inverse, chain_yield=chain_yield, survival=survival, gamma_yield=gamma_yield, sky_weight=sky_weight, sky_blocks=sky_blocks)


def neighbours(field):
    padded = jnp.pad(field, ((0, 0), (1, 1), (1, 1), (1, 1)))
    beside = padded[:, 2:, 1:-1, 1:-1] + padded[:, :-2, 1:-1, 1:-1]
    beside = beside + padded[:, 1:-1, 2:, 1:-1] + padded[:, 1:-1, :-2, 1:-1]
    beside = beside + padded[:, 1:-1, 1:-1, 2:] + padded[:, 1:-1, 1:-1, :-2]
    return beside


def reference(density, space_factor, diff_rate, loss_inverse, chain_yield, survival, gamma_yield, sky_weight, sky_blocks):
    carried = jnp.zeros(density.shape[1:], jnp.float32)
    results = []
    sky = jnp.zeros((NB, PB), jnp.float32)
    onehot = (sky_blocks[:, :, None] == jnp.arange(NB, dtype=jnp.int32)[None, None, :]).astype(jnp.float32)
    for group in range(NG):
        field = density[group]
        rate = diff_rate[group][:, None, None, None] * space_factor[None]
        for step in range(SUBSTEPS):
            field = field + rate * (neighbours(field) - 6.0 * field)
        solved = jnp.dot(loss_inverse[group], field.reshape(P_SIZE, -1), precision=lax.Precision.HIGHEST, preferred_element_type=jnp.float32).reshape(field.shape)
        carried = chain_yield[group][:, None, None, None] * carried + survival[group][:, None, None, None] * solved
        results.append(carried)
        weighted = jnp.dot(gamma_yield[group], carried.reshape(P_SIZE, -1), precision=lax.Precision.HIGHEST, preferred_element_type=jnp.float32)
        emission = (jnp.sum(weighted.reshape(NX, NY, NZ), axis=2) / (P_SIZE * NZ)).astype(jnp.bfloat16)
        columns = emission.reshape(TILES, CX * NY).astype(jnp.float32)
        contribution = jnp.einsum("tc,tlcb->tlb", columns, sky_weight.astype(jnp.float32), precision=lax.Precision.HIGHEST)
        sky = sky + jnp.einsum("tln,tlb->nb", onehot, contribution, precision=lax.Precision.HIGHEST)
    return jnp.stack(results), sky
```

```python
import jax
import jax.numpy as jnp
from jax import lax
from jax.sharding import PartitionSpec as P

SUBSTEPS = 2
NB = 384
HIGH = lax.Precision.HIGHEST


def padded_2(cells, sides, width):
    for axis, dim in sides:
        count = lax.axis_size(axis)
        ends = count - 1
        head = lax.slice_in_dim(cells, 0, width, axis=dim)
        tail = lax.slice_in_dim(cells, cells.shape[dim] - width, cells.shape[dim], axis=dim)
        cells = jnp.concatenate(
            [
                lax.ppermute(tail, axis, [(i, (i + 1) % count) for i in range(ends)]),
                cells,
                lax.ppermute(head, axis, [((i + 1) % count, i) for i in range(ends)]),
            ],
            axis=dim,
        )
    return cells


def from_behind(block, axis, distance):
    devices = range(lax.axis_size(axis))
    route = [(i - distance, i) for i in devices if i - distance in devices]
    return lax.ppermute(block, axis, route)


def cross_sum(field):
    padded = jnp.pad(field, ((0, 0), (0, 0), (1, 1), (1, 1)))
    beside = padded[:, :, 2:, 1:-1] + padded[:, :, :-2, 1:-1]
    beside = beside + padded[:, :, 1:-1, 2:] + padded[:, :, 1:-1, :-2]
    return beside


def emission_weights(chain_all, gamma_all, me):
    groups = chain_all.shape[0]
    g = jnp.arange(groups)[:, None]
    k = jnp.arange(groups)[None, :]
    live = (k > me) & (k <= g)
    factors = jnp.where(live[:, :, None], chain_all[None, :, :], 1.0)
    spread = jnp.prod(factors, axis=1)
    return jnp.where(g >= me, gamma_all * spread, 0.0)


def body(
    density,
    space_factor,
    diff_rate,
    loss_inverse,
    chain_yield,
    survival,
    gamma_yield,
    sky_weight,
    sky_blocks,
):
    tiles = lax.axis_size("space")
    rows = NB // tiles
    params = jnp.stack([chain_yield[0], gamma_yield[0]])
    params_all = lax.all_gather(params, "species")
    blocks_all = lax.all_gather(sky_blocks[0].astype(jnp.float32), "space")

    field = density[0]
    bins = field.shape[0]
    width = field.shape[1]
    depth = field.shape[3]
    rate = diff_rate[0][:, None, None, None]
    factor = rate * space_factor[None]
    for step in range(SUBSTEPS):
        wider = padded_2(field, (("space", 1),), 1)
        beside = wider[:, 2:] + wider[:, :-2] + cross_sum(field)
        field = field + factor * (beside - 6.0 * field)
    solved = jnp.dot(
        loss_inverse[0],
        field.reshape(bins, -1),
        precision=HIGH,
        preferred_element_type=jnp.float32,
    ).reshape(field.shape)
    factor_chain = chain_yield[0][:, None, None, None]
    own_part = survival[0][:, None, None, None] * solved

    me = lax.axis_index("species")
    weights = emission_weights(params_all[:, 0], params_all[:, 1], me)
    own_columns = jnp.sum(own_part, axis=3).reshape(bins, -1)
    partial = jnp.dot(weights, own_columns, precision=HIGH, preferred_element_type=jnp.float32)
    sums = lax.psum(partial, "species")
    emission = (sums / (bins * depth)).astype(jnp.bfloat16).astype(jnp.float32)
    columns = jnp.sum(emission, axis=0)
    contribution = jnp.einsum(
        "c,lcb->lb", columns, sky_weight[0].astype(jnp.float32), precision=HIGH
    )
    gathered = lax.all_gather(contribution, "space")
    lines = gathered.shape[1]
    mine = lax.axis_index("space") * rows + jnp.arange(rows, dtype=jnp.int32)
    onehot = (
        blocks_all.reshape(1, tiles * lines) == mine.astype(jnp.float32)[:, None]
    ).astype(jnp.float32)
    sky = jnp.dot(
        onehot,
        gathered.reshape(tiles * lines, -1),
        precision=HIGH,
        preferred_element_type=jnp.float32,
    )

    carried = own_part
    for section in range(lax.axis_size("species") - 1):
        carried = factor_chain * from_behind(carried, "species", 1) + own_part
    return (carried[None], sky)


def solution(mesh):
    placed = (
        P("species", None, "space", None, None),
        P("space", None, None),
        P("species", None),
        P("species", None, None),
        P("species", None),
        P("species", None),
        P("species", None),
        P("space", None, None, None),
        P("space", None),
    )
    return jax.shard_map(
        body,
        mesh=mesh,
        in_specs=placed,
        out_specs=(P("species", None, "space", None, None), P("space", None)),
        check_vma=False,
    )
```

```python
import jax
import jax.numpy as jnp
from jax import lax
from jax.sharding import PartitionSpec as P

SUBSTEPS = 2
NB = 384
CHUNKS = 4
HIGH = lax.Precision.HIGHEST


def padded_2(cells, sides, width):
    for axis, dim in sides:
        count = lax.axis_size(axis)
        ends = count - 1
        head = lax.slice_in_dim(cells, 0, width, axis=dim)
        tail = lax.slice_in_dim(cells, cells.shape[dim] - width, cells.shape[dim], axis=dim)
        cells = jnp.concatenate(
            [
                lax.ppermute(tail, axis, [(i, (i + 1) % count) for i in range(ends)]),
                cells,
                lax.ppermute(head, axis, [((i + 1) % count, i) for i in range(ends)]),
            ],
            axis=dim,
        )
    return cells


def cross_sum(field):
    padded = jnp.pad(field, ((0, 0), (0, 0), (1, 1), (1, 1)))
    beside = padded[:, :, 2:, 1:-1] + padded[:, :, :-2, 1:-1]
    beside = beside + padded[:, :, 1:-1, 2:] + padded[:, :, 1:-1, :-2]
    return beside


def gather_all(block, axis):
    count = lax.axis_size(axis)
    if count & (count - 1):
        return lax.all_gather(block, axis)
    me = lax.axis_index(axis)
    held = block[None]
    span = 1
    while span < count:
        other = lax.ppermute(held, axis, [(i, i ^ span) for i in range(count)])
        low = (me & span) == 0
        held = jnp.where(
            low,
            jnp.concatenate([held, other], axis=0),
            jnp.concatenate([other, held], axis=0),
        )
        span *= 2
    return held


def body(
    density,
    space_factor,
    diff_rate,
    loss_inverse,
    chain_yield,
    survival,
    gamma_yield,
    sky_weight,
    sky_blocks,
):
    groups = lax.axis_size("species")
    tiles = lax.axis_size("space")
    rows = NB // tiles

    field = density[0]
    bins = field.shape[0]
    depth = field.shape[3]
    rate = diff_rate[0][:, None, None, None]
    factor = rate * space_factor[None]
    for step in range(SUBSTEPS):
        wider = padded_2(field, (("space", 1),), 1)
        beside = wider[:, 2:] + wider[:, :-2] + cross_sum(field)
        field = field + factor * (beside - 6.0 * field)
    solved = jnp.dot(
        loss_inverse[0],
        field.reshape(bins, -1),
        precision=HIGH,
        preferred_element_type=jnp.float32,
    ).reshape(field.shape)
    chain = chain_yield[0]
    own_part = survival[0][:, None, None, None] * solved

    own_columns = jnp.sum(own_part, axis=3).reshape(bins, -1)
    cols = own_columns.shape[1]
    packed = jnp.concatenate(
        [own_columns, jnp.concatenate([chain, gamma_yield[0]]).reshape(1, -1)[:, :cols]], axis=0
    ) if cols == 2 * bins else None
    everyone = gather_all(packed, "species")
    sums = everyone[0, :bins]
    total = jnp.zeros((cols,), jnp.float32)
    for group in range(groups):
        if group > 0:
            sums = everyone[group, bins, :bins][:, None] * sums + everyone[group, :bins]
        weighted = jnp.dot(
            everyone[group, bins, bins:], sums, precision=HIGH, preferred_element_type=jnp.float32
        )
        emission = lax.reduce_precision(weighted / (bins * depth), exponent_bits=8, mantissa_bits=7)
        total = total + emission
    contribution = jnp.einsum(
        "c,lcb->lb", total, sky_weight[0].astype(jnp.float32), precision=HIGH
    )
    lines, pixels = contribution.shape
    ids = jnp.zeros((1, pixels), jnp.float32).at[0, :lines].set(sky_blocks[0].astype(jnp.float32))
    gathered = gather_all(jnp.concatenate([contribution, ids], axis=0), "space")
    mine = lax.axis_index("space") * rows + jnp.arange(rows, dtype=jnp.int32)
    onehot = (
        gathered[:, lines, :lines].reshape(1, tiles * lines) == mine.astype(jnp.float32)[:, None]
    ).astype(jnp.float32)
    sky = jnp.dot(
        onehot,
        gathered[:, :lines].reshape(tiles * lines, pixels),
        precision=HIGH,
        preferred_element_type=jnp.float32,
    )

    base = bins // CHUNKS
    bounds = [0]
    for c in range(CHUNKS):
        bounds.append(bounds[-1] + base + 2 * c - (CHUNKS - 1))
    bounds[-1] = bins
    pieces = [own_part[bounds[c]:bounds[c + 1]] for c in range(CHUNKS)]
    scales = [chain[bounds[c]:bounds[c + 1]][:, None, None, None] for c in range(CHUNKS)]
    for wave in range(CHUNKS + groups - 2):
        for c in range(CHUNKS):
            s = wave - c
            if 0 <= s < groups - 1:
                arrived = lax.ppermute(pieces[c], "species", [(s, s + 1)])
                pieces[c] = pieces[c] + scales[c] * arrived
    carried = jnp.concatenate(pieces, axis=0)
    return (carried[None], sky)


def solution(mesh):
    placed = (
        P("species", None, "space", None, None),
        P("space", None, None),
        P("species", None),
        P("species", None, None),
        P("species", None),
        P("species", None),
        P("species", None),
        P("space", None, None, None),
        P("space", None),
    )
    return jax.shard_map(
        body,
        mesh=mesh,
        in_specs=placed,
        out_specs=(P("species", None, "space", None, None), P("space", None)),
        check_vma=False,
    )
```

```python
import jax
import jax.numpy as jnp
from jax import lax
from jax.sharding import PartitionSpec as P

SUBSTEPS = 2
NB = 384
CHUNKS = 4
HIGH = lax.Precision.HIGHEST


def padded_2(cells, sides, width):
    for axis, dim in sides:
        count = lax.axis_size(axis)
        ends = count - 1
        head = lax.slice_in_dim(cells, 0, width, axis=dim)
        tail = lax.slice_in_dim(cells, cells.shape[dim] - width, cells.shape[dim], axis=dim)
        cells = jnp.concatenate(
            [
                lax.ppermute(tail, axis, [(i, (i + 1) % count) for i in range(ends)]),
                cells,
                lax.ppermute(head, axis, [((i + 1) % count, i) for i in range(ends)]),
            ],
            axis=dim,
        )
    return cells


def cross_sum(field):
    padded = jnp.pad(field, ((0, 0), (0, 0), (1, 1), (1, 1)))
    beside = padded[:, :, 2:, 1:-1] + padded[:, :, :-2, 1:-1]
    beside = beside + padded[:, :, 1:-1, 2:] + padded[:, :, 1:-1, :-2]
    return beside


def gather_all(block, axis):
    count = lax.axis_size(axis)
    if count & (count - 1):
        return lax.all_gather(block, axis)
    me = lax.axis_index(axis)
    held = block[None]
    span = 1
    while span < count:
        other = lax.ppermute(held, axis, [(i, i ^ span) for i in range(count)])
        low = (me & span) == 0
        held = jnp.where(
            low,
            jnp.concatenate([held, other], axis=0),
            jnp.concatenate([other, held], axis=0),
        )
        span *= 2
    return held


def body(
    density,
    space_factor,
    diff_rate,
    loss_inverse,
    chain_yield,
    survival,
    gamma_yield,
    sky_weight,
    sky_blocks,
):
    groups = lax.axis_size("species")
    tiles = lax.axis_size("space")
    rows = NB // tiles

    field = density[0]
    bins = field.shape[0]
    depth = field.shape[3]
    rate = diff_rate[0][:, None, None, None]
    factor = rate * space_factor[None]
    for step in range(SUBSTEPS):
        wider = padded_2(field, (("space", 1),), 1)
        beside = wider[:, 2:] + wider[:, :-2] + cross_sum(field)
        field = field + factor * (beside - 6.0 * field)
    solved = jnp.dot(
        loss_inverse[0],
        field.reshape(bins, -1),
        precision=HIGH,
        preferred_element_type=jnp.float32,
    ).reshape(field.shape)
    chain = chain_yield[0]
    own_part = survival[0][:, None, None, None] * solved

    own_columns = jnp.sum(own_part, axis=3).reshape(bins, -1)
    cols = own_columns.shape[1]
    extra = jnp.zeros((2, cols), jnp.float32).at[0, :bins].set(chain).at[1, :bins].set(gamma_yield[0])
    packed = jnp.concatenate([own_columns, extra], axis=0)
    me_g = lax.axis_index("species")
    everyone = packed[None]
    span = 1
    while span < groups:
        other = lax.ppermute(everyone, "species", [(i, i ^ span) for i in range(groups)])
        if span == 1:
            own_part, other = lax.optimization_barrier((own_part, other))
        low = (me_g & span) == 0
        everyone = jnp.where(
            low,
            jnp.concatenate([everyone, other], axis=0),
            jnp.concatenate([other, everyone], axis=0),
        )
        span *= 2
    sums = everyone[0, :bins]
    total = jnp.zeros((cols,), jnp.float32)
    for group in range(groups):
        if group > 0:
            sums = everyone[group, bins, :bins][:, None] * sums + everyone[group, :bins]
        weighted = jnp.dot(
            everyone[group, bins + 1, :bins], sums, precision=HIGH, preferred_element_type=jnp.float32
        )
        emission = lax.reduce_precision(weighted / (bins * depth), exponent_bits=8, mantissa_bits=7)
        total = total + emission
    contribution = jnp.einsum(
        "c,lcb->lb", total, sky_weight[0].astype(jnp.float32), precision=HIGH
    )
    lines, pixels = contribution.shape
    ids = jnp.zeros((1, pixels), jnp.float32).at[0, :lines].set(sky_blocks[0].astype(jnp.float32))
    payload = jnp.concatenate([contribution, ids], axis=0)
    base = bins // CHUNKS
    bounds = [0]
    for c in range(CHUNKS):
        bounds.append(bounds[-1] + base + 2 * c - (CHUNKS - 1))
    bounds[-1] = bins
    pieces = [own_part[bounds[c]:bounds[c + 1]] for c in range(CHUNKS)]
    scales = [chain[bounds[c]:bounds[c + 1]][:, None, None, None] for c in range(CHUNKS)]
    for wave in range(CHUNKS + groups - 2):
        for c in range(CHUNKS):
            s = wave - c
            if 0 <= s < groups - 1:
                arrived = lax.ppermute(pieces[c], "species", [(s, s + 1)])
                if wave == 0:
                    payload, arrived = lax.optimization_barrier((payload, arrived))
                pieces[c] = pieces[c] + scales[c] * arrived
    carried = jnp.concatenate(pieces, axis=0)
    gathered = gather_all(payload, "space")
    mine = lax.axis_index("space") * rows + jnp.arange(rows, dtype=jnp.int32)
    onehot = (
        gathered[:, lines, :lines].reshape(1, tiles * lines) == mine.astype(jnp.float32)[:, None]
    ).astype(jnp.float32)
    sky = jnp.dot(
        onehot,
        gathered[:, :lines].reshape(tiles * lines, pixels),
        precision=HIGH,
        preferred_element_type=jnp.float32,
    )

    return (carried[None], sky)


def solution(mesh):
    placed = (
        P("species", None, "space", None, None),
        P("space", None, None),
        P("species", None),
        P("species", None, None),
        P("species", None),
        P("species", None),
        P("species", None),
        P("space", None, None, None),
        P("space", None),
    )
    return jax.shard_map(
        body,
        mesh=mesh,
        in_specs=placed,
        out_specs=(P("species", None, "space", None, None), P("space", None)),
        check_vma=False,
    )
```

```python
import jax
import jax.numpy as jnp
from jax import lax
from jax.sharding import PartitionSpec as P

SUBSTEPS = 2
NB = 384
CHUNKS = 4
HIGH = lax.Precision.HIGHEST


def padded_2(cells, sides, width):
    for axis, dim in sides:
        count = lax.axis_size(axis)
        ends = count - 1
        head = lax.slice_in_dim(cells, 0, width, axis=dim)
        tail = lax.slice_in_dim(cells, cells.shape[dim] - width, cells.shape[dim], axis=dim)
        cells = jnp.concatenate(
            [
                lax.ppermute(tail, axis, [(i, (i + 1) % count) for i in range(ends)]),
                cells,
                lax.ppermute(head, axis, [((i + 1) % count, i) for i in range(ends)]),
            ],
            axis=dim,
        )
    return cells


def cross_sum(field):
    padded = jnp.pad(field, ((0, 0), (0, 0), (1, 1), (1, 1)))
    beside = padded[:, :, 2:, 1:-1] + padded[:, :, :-2, 1:-1]
    beside = beside + padded[:, :, 1:-1, 2:] + padded[:, :, 1:-1, :-2]
    return beside


def gather_all(block, axis):
    count = lax.axis_size(axis)
    if count & (count - 1):
        return lax.all_gather(block, axis)
    me = lax.axis_index(axis)
    held = block[None]
    span = 1
    while span < count:
        other = lax.ppermute(held, axis, [(i, i ^ span) for i in range(count)])
        low = (me & span) == 0
        held = jnp.where(
            low,
            jnp.concatenate([held, other], axis=0),
            jnp.concatenate([other, held], axis=0),
        )
        span *= 2
    return held


def body(
    density,
    space_factor,
    diff_rate,
    loss_inverse,
    chain_yield,
    survival,
    gamma_yield,
    sky_weight,
    sky_blocks,
):
    groups = lax.axis_size("species")
    tiles = lax.axis_size("space")
    rows = NB // tiles

    field = density[0]
    bins = field.shape[0]
    depth = field.shape[3]
    rate = diff_rate[0][:, None, None, None]
    factor = rate * space_factor[None]
    halo = SUBSTEPS
    count = lax.axis_size("space")
    mine = jnp.concatenate([field, space_factor[None]], axis=0)
    from_left = lax.ppermute(
        mine[:, mine.shape[1] - halo:], "space", [(i, i + 1) for i in range(count - 1)]
    )
    from_right = lax.ppermute(mine[:, :halo], "space", [(i + 1, i) for i in range(count - 1)])
    wide = jnp.concatenate([from_left[:bins], field, from_right[:bins]], axis=1)
    wide_factor = rate * jnp.concatenate([from_left[bins], space_factor, from_right[bins]], axis=0)[None]
    for step in range(SUBSTEPS):
        inner = wide[:, 1:-1]
        beside = wide[:, 2:] + wide[:, :-2] + cross_sum(inner)
        wide = inner + wide_factor[:, 1 + step:wide_factor.shape[1] - 1 - step] * (beside - 6.0 * inner)
    field = wide
    solved = jnp.dot(
        loss_inverse[0],
        field.reshape(bins, -1),
        precision=HIGH,
        preferred_element_type=jnp.float32,
    ).reshape(field.shape)
    chain = chain_yield[0]
    own_part = survival[0][:, None, None, None] * solved

    own_columns = jnp.sum(own_part, axis=3).reshape(bins, -1)
    cols = own_columns.shape[1]
    extra = jnp.zeros((2, cols), jnp.float32).at[0, :bins].set(chain).at[1, :bins].set(gamma_yield[0])
    packed = jnp.concatenate([own_columns, extra], axis=0)
    me_g = lax.axis_index("species")
    everyone = packed[None]
    span = 1
    while span < groups:
        other = lax.ppermute(everyone, "species", [(i, i ^ span) for i in range(groups)])
        if span == 1:
            own_part, other = lax.optimization_barrier((own_part, other))
        low = (me_g & span) == 0
        everyone = jnp.where(
            low,
            jnp.concatenate([everyone, other], axis=0),
            jnp.concatenate([other, everyone], axis=0),
        )
        span *= 2
    sums = everyone[0, :bins]
    total = jnp.zeros((cols,), jnp.float32)
    for group in range(groups):
        if group > 0:
            sums = everyone[group, bins, :bins][:, None] * sums + everyone[group, :bins]
        weighted = jnp.dot(
            everyone[group, bins + 1, :bins], sums, precision=HIGH, preferred_element_type=jnp.float32
        )
        emission = lax.reduce_precision(weighted / (bins * depth), exponent_bits=8, mantissa_bits=7)
        total = total + emission
    contribution = jnp.einsum(
        "c,lcb->lb", total, sky_weight[0].astype(jnp.float32), precision=HIGH
    )
    lines, pixels = contribution.shape
    ids = jnp.zeros((1, pixels), jnp.float32).at[0, :lines].set(sky_blocks[0].astype(jnp.float32))
    payload = jnp.concatenate([contribution, ids], axis=0)
    base = bins // CHUNKS
    bounds = [0]
    for c in range(CHUNKS):
        bounds.append(bounds[-1] + base + 2 * c - (CHUNKS - 1))
    bounds[-1] = bins
    pieces = [own_part[bounds[c]:bounds[c + 1]] for c in range(CHUNKS)]
    scales = [chain[bounds[c]:bounds[c + 1]][:, None, None, None] for c in range(CHUNKS)]
    for wave in range(CHUNKS + groups - 2):
        for c in range(CHUNKS):
            s = wave - c
            if 0 <= s < groups - 1:
                arrived = lax.ppermute(pieces[c], "species", [(s, s + 1)])
                if wave == 0:
                    payload, arrived = lax.optimization_barrier((payload, arrived))
                pieces[c] = pieces[c] + scales[c] * arrived
    carried = jnp.concatenate(pieces, axis=0)
    gathered = gather_all(payload, "space")
    mine = lax.axis_index("space") * rows + jnp.arange(rows, dtype=jnp.int32)
    onehot = (
        gathered[:, lines, :lines].reshape(1, tiles * lines) == mine.astype(jnp.float32)[:, None]
    ).astype(jnp.float32)
    sky = jnp.dot(
        onehot,
        gathered[:, :lines].reshape(tiles * lines, pixels),
        precision=HIGH,
        preferred_element_type=jnp.float32,
    )

    return (carried[None], sky)


def solution(mesh):
    placed = (
        P("species", None, "space", None, None),
        P("space", None, None),
        P("species", None),
        P("species", None, None),
        P("species", None),
        P("species", None),
        P("species", None),
        P("space", None, None, None),
        P("space", None),
    )
    return jax.shard_map(
        body,
        mesh=mesh,
        in_specs=placed,
        out_specs=(P("species", None, "space", None, None), P("space", None)),
        check_vma=False,
    )
```

```python
import jax
import jax.numpy as jnp
from jax import lax
from jax.sharding import PartitionSpec as P

SUBSTEPS = 2
NB = 384
CHUNKS = 4
HIGH = lax.Precision.HIGHEST


def padded_2(cells, sides, width):
    for axis, dim in sides:
        count = lax.axis_size(axis)
        ends = count - 1
        head = lax.slice_in_dim(cells, 0, width, axis=dim)
        tail = lax.slice_in_dim(cells, cells.shape[dim] - width, cells.shape[dim], axis=dim)
        cells = jnp.concatenate(
            [
                lax.ppermute(tail, axis, [(i, (i + 1) % count) for i in range(ends)]),
                cells,
                lax.ppermute(head, axis, [((i + 1) % count, i) for i in range(ends)]),
            ],
            axis=dim,
        )
    return cells


def cross_sum(field):
    padded = jnp.pad(field, ((0, 0), (0, 0), (1, 1), (1, 1)))
    beside = padded[:, :, 2:, 1:-1] + padded[:, :, :-2, 1:-1]
    beside = beside + padded[:, :, 1:-1, 2:] + padded[:, :, 1:-1, :-2]
    return beside


def gather_all(block, axis):
    count = lax.axis_size(axis)
    if count & (count - 1):
        return lax.all_gather(block, axis)
    me = lax.axis_index(axis)
    held = block[None]
    span = 1
    while span < count:
        other = lax.ppermute(held, axis, [(i, i ^ span) for i in range(count)])
        low = (me & span) == 0
        held = jnp.where(
            low,
            jnp.concatenate([held, other], axis=0),
            jnp.concatenate([other, held], axis=0),
        )
        span *= 2
    return held


def body(
    density,
    space_factor,
    diff_rate,
    loss_inverse,
    chain_yield,
    survival,
    gamma_yield,
    sky_weight,
    sky_blocks,
):
    groups = lax.axis_size("species")
    tiles = lax.axis_size("space")
    rows = NB // tiles

    field = density[0]
    bins = field.shape[0]
    depth = field.shape[3]
    rate = diff_rate[0][:, None, None, None]
    chain = chain_yield[0]
    halo = SUBSTEPS
    count = lax.axis_size("space")
    right_pairs = [(i, i + 1) for i in range(count - 1)]
    left_pairs = [(i + 1, i) for i in range(count - 1)]
    layers = field.shape[1]
    factor_left = lax.ppermute(space_factor[layers - halo:], "space", right_pairs)
    factor_right = lax.ppermute(space_factor[:halo], "space", left_pairs)
    wide_space = jnp.concatenate([factor_left, space_factor, factor_right], axis=0)[None]

    base = bins // CHUNKS
    sizes = [base + 2 * c - (CHUNKS - 1) for c in range(CHUNKS)]
    sizes[-1] += bins - sum(sizes)
    tops = [bins]
    for size in sizes:
        tops.append(tops[-1] - size)
    spans = [(tops[c + 1], tops[c]) for c in range(CHUNKS)]

    diffused = []
    pieces = []
    scales = []
    for low, high in spans:
        block = field[low:high]
        from_left = lax.ppermute(block[:, layers - halo:], "space", right_pairs)
        from_right = lax.ppermute(block[:, :halo], "space", left_pairs)
        wide = jnp.concatenate([from_left, block, from_right], axis=1)
        wide_factor = rate[low:high] * wide_space
        for step in range(SUBSTEPS):
            inner = wide[:, 1:-1]
            beside = wide[:, 2:] + wide[:, :-2] + cross_sum(inner)
            wide = inner + wide_factor[:, 1 + step:wide_factor.shape[1] - 1 - step] * (beside - 6.0 * inner)
        diffused.insert(0, wide)
        above = jnp.concatenate(diffused, axis=0) if len(diffused) > 1 else wide
        solved = jnp.dot(
            loss_inverse[0, low:high, low:],
            above.reshape(bins - low, -1),
            precision=HIGH,
            preferred_element_type=jnp.float32,
        ).reshape(wide.shape)
        pieces.append(survival[0, low:high][:, None, None, None] * solved)
        scales.append(chain[low:high][:, None, None, None])
    own_part = jnp.concatenate(pieces[::-1], axis=0)

    for c in range(CHUNKS):
        arrived = lax.ppermute(pieces[c], "species", [(0, 1)])
        pieces[c] = pieces[c] + scales[c] * arrived
        if c == CHUNKS - 2:
            early = pieces[:CHUNKS - 1]
    own_columns = jnp.sum(own_part, axis=3).reshape(bins, -1)
    cols = own_columns.shape[1]
    extra = jnp.zeros((2, cols), jnp.float32).at[0, :bins].set(chain).at[1, :bins].set(gamma_yield[0])
    packed = jnp.concatenate([own_columns, extra], axis=0)
    packed, early = lax.optimization_barrier((packed, early))
    pieces[:CHUNKS - 1] = early
    me_g = lax.axis_index("species")
    everyone = packed[None]
    span = 1
    while span < groups:
        other = lax.ppermute(everyone, "species", [(i, i ^ span) for i in range(groups)])
        low = (me_g & span) == 0
        everyone = jnp.where(
            low,
            jnp.concatenate([everyone, other], axis=0),
            jnp.concatenate([other, everyone], axis=0),
        )
        span *= 2
    sums = everyone[0, :bins]
    total = jnp.zeros((cols,), jnp.float32)
    for group in range(groups):
        if group > 0:
            sums = everyone[group, bins, :bins][:, None] * sums + everyone[group, :bins]
        weighted = jnp.dot(
            everyone[group, bins + 1, :bins], sums, precision=HIGH, preferred_element_type=jnp.float32
        )
        emission = lax.reduce_precision(weighted / (bins * depth), exponent_bits=8, mantissa_bits=7)
        total = total + emission
    contribution = jnp.einsum(
        "c,lcb->lb", total, sky_weight[0].astype(jnp.float32), precision=HIGH
    )
    lines, pixels = contribution.shape
    ids = jnp.zeros((1, pixels), jnp.float32).at[0, :lines].set(sky_blocks[0].astype(jnp.float32))
    payload = jnp.concatenate([contribution, ids], axis=0)
    for wave in range(CHUNKS + groups - 2):
        for c in range(CHUNKS):
            s = wave - c
            if 1 <= s < groups - 1:
                arrived = lax.ppermute(pieces[c], "species", [(s, s + 1)])
                pieces[c] = pieces[c] + scales[c] * arrived
    carried = jnp.concatenate(pieces[::-1], axis=0)
    gathered = gather_all(payload, "space")
    mine = lax.axis_index("space") * rows + jnp.arange(rows, dtype=jnp.int32)
    onehot = (
        gathered[:, lines, :lines].reshape(1, tiles * lines) == mine.astype(jnp.float32)[:, None]
    ).astype(jnp.float32)
    sky = jnp.dot(
        onehot,
        gathered[:, :lines].reshape(tiles * lines, pixels),
        precision=HIGH,
        preferred_element_type=jnp.float32,
    )

    return (carried[None], sky)


def solution(mesh):
    placed = (
        P("species", None, "space", None, None),
        P("space", None, None),
        P("species", None),
        P("species", None, None),
        P("species", None),
        P("species", None),
        P("species", None),
        P("space", None, None, None),
        P("space", None),
    )
    return jax.shard_map(
        body,
        mesh=mesh,
        in_specs=placed,
        out_specs=(P("species", None, "space", None, None), P("space", None)),
        check_vma=False,
    )
```

```python
import jax
import jax.numpy as jnp
from jax import lax
from jax.sharding import PartitionSpec as P

SUBSTEPS = 2
NB = 384
CHUNKS = 4
HIGH = lax.Precision.HIGHEST


def padded_2(cells, sides, width):
    for axis, dim in sides:
        count = lax.axis_size(axis)
        ends = count - 1
        head = lax.slice_in_dim(cells, 0, width, axis=dim)
        tail = lax.slice_in_dim(cells, cells.shape[dim] - width, cells.shape[dim], axis=dim)
        cells = jnp.concatenate(
            [
                lax.ppermute(tail, axis, [(i, (i + 1) % count) for i in range(ends)]),
                cells,
                lax.ppermute(head, axis, [((i + 1) % count, i) for i in range(ends)]),
            ],
            axis=dim,
        )
    return cells


def cross_sum(field):
    padded = jnp.pad(field, ((0, 0), (0, 0), (1, 1), (1, 1)))
    beside = padded[:, :, 2:, 1:-1] + padded[:, :, :-2, 1:-1]
    beside = beside + padded[:, :, 1:-1, 2:] + padded[:, :, 1:-1, :-2]
    return beside


def gather_all(block, axis):
    count = lax.axis_size(axis)
    if count & (count - 1):
        return lax.all_gather(block, axis)
    me = lax.axis_index(axis)
    held = block[None]
    span = 1
    while span < count:
        other = lax.ppermute(held, axis, [(i, i ^ span) for i in range(count)])
        low = (me & span) == 0
        held = jnp.where(
            low,
            jnp.concatenate([held, other], axis=0),
            jnp.concatenate([other, held], axis=0),
        )
        span *= 2
    return held


def body(
    density,
    space_factor,
    diff_rate,
    loss_inverse,
    chain_yield,
    survival,
    gamma_yield,
    sky_weight,
    sky_blocks,
):
    groups = lax.axis_size("species")
    tiles = lax.axis_size("space")
    rows = NB // tiles

    field = density[0]
    bins = field.shape[0]
    depth = field.shape[3]
    rate = diff_rate[0][:, None, None, None]
    factor = rate * space_factor[None]
    halo = SUBSTEPS
    count = lax.axis_size("space")
    mine = jnp.concatenate([field, space_factor[None]], axis=0)
    from_left = lax.ppermute(
        mine[:, mine.shape[1] - halo:], "space", [(i, i + 1) for i in range(count - 1)]
    )
    from_right = lax.ppermute(mine[:, :halo], "space", [(i + 1, i) for i in range(count - 1)])
    wide = jnp.concatenate([from_left[:bins], field, from_right[:bins]], axis=1)
    wide_factor = rate * jnp.concatenate([from_left[bins], space_factor, from_right[bins]], axis=0)[None]
    for step in range(SUBSTEPS):
        inner = wide[:, 1:-1]
        beside = wide[:, 2:] + wide[:, :-2] + cross_sum(inner)
        wide = inner + wide_factor[:, 1 + step:wide_factor.shape[1] - 1 - step] * (beside - 6.0 * inner)
    field = wide
    solved = jnp.dot(
        loss_inverse[0],
        field.reshape(bins, -1),
        precision=HIGH,
        preferred_element_type=jnp.float32,
    ).reshape(field.shape)
    chain = chain_yield[0]
    own_part = survival[0][:, None, None, None] * solved

    own_columns = jnp.sum(own_part, axis=3).reshape(bins, -1)
    cols = own_columns.shape[1]
    extra = jnp.zeros((2, cols), jnp.float32).at[0, :bins].set(chain).at[1, :bins].set(gamma_yield[0])
    packed = jnp.concatenate([own_columns, extra], axis=0)
    me_g = lax.axis_index("species")
    everyone = packed[None]
    span = 1
    while span < groups:
        other = lax.ppermute(everyone, "species", [(i, i ^ span) for i in range(groups)])
        if span == 1:
            own_part, other = lax.optimization_barrier((own_part, other))
        low = (me_g & span) == 0
        everyone = jnp.where(
            low,
            jnp.concatenate([everyone, other], axis=0),
            jnp.concatenate([other, everyone], axis=0),
        )
        span *= 2
    sums = everyone[0, :bins]
    total = jnp.zeros((cols,), jnp.float32)
    for group in range(groups):
        if group > 0:
            sums = everyone[group, bins, :bins][:, None] * sums + everyone[group, :bins]
        weighted = jnp.dot(
            everyone[group, bins + 1, :bins], sums, precision=HIGH, preferred_element_type=jnp.float32
        )
        emission = lax.reduce_precision(weighted / (bins * depth), exponent_bits=8, mantissa_bits=7)
        total = total + emission
    contribution = jnp.einsum(
        "c,lcb->lb", total, sky_weight[0].astype(jnp.float32), precision=HIGH
    )
    lines, pixels = contribution.shape
    ids = jnp.zeros((1, pixels), jnp.float32).at[0, :lines].set(sky_blocks[0].astype(jnp.float32))
    payload = jnp.concatenate([contribution, ids], axis=0)
    base = bins // CHUNKS
    bounds = [0]
    for c in range(CHUNKS):
        bounds.append(bounds[-1] + base + (CHUNKS - 1) - 2 * c)
    bounds[-1] = bins
    pieces = [own_part[bounds[c]:bounds[c + 1]] for c in range(CHUNKS)]
    scales = [chain[bounds[c]:bounds[c + 1]][:, None, None, None] for c in range(CHUNKS)]
    for wave in range(CHUNKS + groups - 2):
        for c in range(CHUNKS):
            s = wave - c
            if 0 <= s < groups - 1:
                arrived = lax.ppermute(pieces[c], "species", [(s, s + 1)])
                if wave == 0:
                    payload, arrived = lax.optimization_barrier((payload, arrived))
                pieces[c] = pieces[c] + scales[c] * arrived
    carried = jnp.concatenate(pieces, axis=0)
    gathered = gather_all(payload, "space")
    mine = lax.axis_index("space") * rows + jnp.arange(rows, dtype=jnp.int32)
    onehot = (
        gathered[:, lines, :lines].reshape(1, tiles * lines) == mine.astype(jnp.float32)[:, None]
    ).astype(jnp.float32)
    sky = jnp.dot(
        onehot,
        gathered[:, :lines].reshape(tiles * lines, pixels),
        precision=HIGH,
        preferred_element_type=jnp.float32,
    )

    return (carried[None], sky)


def solution(mesh):
    placed = (
        P("species", None, "space", None, None),
        P("space", None, None),
        P("species", None),
        P("species", None, None),
        P("species", None),
        P("species", None),
        P("species", None),
        P("space", None, None, None),
        P("space", None),
    )
    return jax.shard_map(
        body,
        mesh=mesh,
        in_specs=placed,
        out_specs=(P("species", None, "space", None, None), P("space", None)),
        check_vma=False,
    )
```

```python
import jax
import jax.numpy as jnp
from jax import lax
from jax.sharding import PartitionSpec as P

SUBSTEPS = 2
NB = 384
CHUNKS = 4
HIGH = lax.Precision.HIGHEST


def padded_2(cells, sides, width):
    for axis, dim in sides:
        count = lax.axis_size(axis)
        ends = count - 1
        head = lax.slice_in_dim(cells, 0, width, axis=dim)
        tail = lax.slice_in_dim(cells, cells.shape[dim] - width, cells.shape[dim], axis=dim)
        cells = jnp.concatenate(
            [
                lax.ppermute(tail, axis, [(i, (i + 1) % count) for i in range(ends)]),
                cells,
                lax.ppermute(head, axis, [((i + 1) % count, i) for i in range(ends)]),
            ],
            axis=dim,
        )
    return cells


def cross_sum(field):
    padded = jnp.pad(field, ((0, 0), (0, 0), (1, 1), (1, 1)))
    beside = padded[:, :, 2:, 1:-1] + padded[:, :, :-2, 1:-1]
    beside = beside + padded[:, :, 1:-1, 2:] + padded[:, :, 1:-1, :-2]
    return beside


def gather_all(block, axis):
    count = lax.axis_size(axis)
    if count & (count - 1):
        return lax.all_gather(block, axis)
    me = lax.axis_index(axis)
    held = block[None]
    span = 1
    while span < count:
        other = lax.ppermute(held, axis, [(i, i ^ span) for i in range(count)])
        low = (me & span) == 0
        held = jnp.where(
            low,
            jnp.concatenate([held, other], axis=0),
            jnp.concatenate([other, held], axis=0),
        )
        span *= 2
    return held


def body(
    density,
    space_factor,
    diff_rate,
    loss_inverse,
    chain_yield,
    survival,
    gamma_yield,
    sky_weight,
    sky_blocks,
):
    groups = lax.axis_size("species")
    tiles = lax.axis_size("space")
    rows = NB // tiles

    field = density[0]
    bins = field.shape[0]
    depth = field.shape[3]
    rate = diff_rate[0][:, None, None, None]
    factor = rate * space_factor[None]
    halo = SUBSTEPS
    count = lax.axis_size("space")
    mine = jnp.concatenate([field, space_factor[None]], axis=0)
    from_left = lax.ppermute(
        mine[:, mine.shape[1] - halo:], "space", [(i, i + 1) for i in range(count - 1)]
    )
    from_right = lax.ppermute(mine[:, :halo], "space", [(i + 1, i) for i in range(count - 1)])
    wide = jnp.concatenate([from_left[:bins], field, from_right[:bins]], axis=1)
    wide_factor = rate * jnp.concatenate([from_left[bins], space_factor, from_right[bins]], axis=0)[None]
    for step in range(SUBSTEPS):
        inner = wide[:, 1:-1]
        beside = wide[:, 2:] + wide[:, :-2] + cross_sum(inner)
        wide = inner + wide_factor[:, 1 + step:wide_factor.shape[1] - 1 - step] * (beside - 6.0 * inner)
    field = wide
    solved = jnp.dot(
        loss_inverse[0],
        field.reshape(bins, -1),
        precision=HIGH,
        preferred_element_type=jnp.float32,
    ).reshape(field.shape)
    chain = chain_yield[0]
    own_part = survival[0][:, None, None, None] * solved

    own_columns = jnp.sum(own_part, axis=3).reshape(bins, -1)
    cols = own_columns.shape[1]
    extra = jnp.zeros((2, cols), jnp.float32).at[0, :bins].set(chain).at[1, :bins].set(gamma_yield[0])
    packed = jnp.concatenate([own_columns, extra], axis=0)
    me_g = lax.axis_index("species")
    everyone = packed[None]
    span = 1
    while span < groups:
        other = lax.ppermute(everyone, "species", [(i, i ^ span) for i in range(groups)])
        if span == 1:
            own_part, other = lax.optimization_barrier((own_part, other))
        low = (me_g & span) == 0
        everyone = jnp.where(
            low,
            jnp.concatenate([everyone, other], axis=0),
            jnp.concatenate([other, everyone], axis=0),
        )
        span *= 2
    sums = everyone[0, :bins]
    total = jnp.zeros((cols,), jnp.float32)
    for group in range(groups):
        if group > 0:
            sums = everyone[group, bins, :bins][:, None] * sums + everyone[group, :bins]
        weighted = jnp.dot(
            everyone[group, bins + 1, :bins], sums, precision=HIGH, preferred_element_type=jnp.float32
        )
        emission = lax.reduce_precision(weighted / (bins * depth), exponent_bits=8, mantissa_bits=7)
        total = total + emission
    contribution = jnp.einsum(
        "c,lcb->lb", total, sky_weight[0].astype(jnp.float32), precision=HIGH
    )
    lines, pixels = contribution.shape
    ids = jnp.zeros((1, pixels), jnp.float32).at[0, :lines].set(sky_blocks[0].astype(jnp.float32))
    payload = jnp.concatenate([contribution, ids], axis=0)
    base = bins // CHUNKS
    bounds = [0]
    for c in range(CHUNKS):
        bounds.append(bounds[-1] + base + 2 * c - (CHUNKS - 1))
    bounds[-1] = bins
    pieces = [own_part[bounds[c]:bounds[c + 1]] for c in range(CHUNKS)]
    scales = [chain[bounds[c]:bounds[c + 1]][:, None, None, None] for c in range(CHUNKS)]
    for wave in range(CHUNKS + groups - 2):
        for c in range(CHUNKS):
            s = wave - c
            if 0 <= s < groups - 1:
                arrived = lax.ppermute(pieces[c], "species", [(s, s + 1)])
                if s == 0 and c == CHUNKS - 1:
                    payload, arrived = lax.optimization_barrier((payload, arrived))
                pieces[c] = pieces[c] + scales[c] * arrived
    carried = jnp.concatenate(pieces, axis=0)
    gathered = gather_all(payload, "space")
    mine = lax.axis_index("space") * rows + jnp.arange(rows, dtype=jnp.int32)
    onehot = (
        gathered[:, lines, :lines].reshape(1, tiles * lines) == mine.astype(jnp.float32)[:, None]
    ).astype(jnp.float32)
    sky = jnp.dot(
        onehot,
        gathered[:, :lines].reshape(tiles * lines, pixels),
        precision=HIGH,
        preferred_element_type=jnp.float32,
    )

    return (carried[None], sky)


def solution(mesh):
    placed = (
        P("species", None, "space", None, None),
        P("space", None, None),
        P("species", None),
        P("species", None, None),
        P("species", None),
        P("species", None),
        P("species", None),
        P("space", None, None, None),
        P("space", None),
    )
    return jax.shard_map(
        body,
        mesh=mesh,
        in_specs=placed,
        out_specs=(P("species", None, "space", None, None), P("space", None)),
        check_vma=False,
    )
```

```python
import jax
import jax.numpy as jnp
from jax import lax
from jax.sharding import PartitionSpec as P

SUBSTEPS = 2
NB = 384
CHUNKS = 4
HIGH = lax.Precision.HIGHEST


def padded_2(cells, sides, width):
    for axis, dim in sides:
        count = lax.axis_size(axis)
        ends = count - 1
        head = lax.slice_in_dim(cells, 0, width, axis=dim)
        tail = lax.slice_in_dim(cells, cells.shape[dim] - width, cells.shape[dim], axis=dim)
        cells = jnp.concatenate(
            [
                lax.ppermute(tail, axis, [(i, (i + 1) % count) for i in range(ends)]),
                cells,
                lax.ppermute(head, axis, [((i + 1) % count, i) for i in range(ends)]),
            ],
            axis=dim,
        )
    return cells


def cross_sum(field):
    padded = jnp.pad(field, ((0, 0), (0, 0), (1, 1), (1, 1)))
    beside = padded[:, :, 2:, 1:-1] + padded[:, :, :-2, 1:-1]
    beside = beside + padded[:, :, 1:-1, 2:] + padded[:, :, 1:-1, :-2]
    return beside


def gather_all(block, axis):
    count = lax.axis_size(axis)
    if count & (count - 1):
        return lax.all_gather(block, axis)
    me = lax.axis_index(axis)
    held = block[None]
    span = 1
    while span < count:
        other = lax.ppermute(held, axis, [(i, i ^ span) for i in range(count)])
        low = (me & span) == 0
        held = jnp.where(
            low,
            jnp.concatenate([held, other], axis=0),
            jnp.concatenate([other, held], axis=0),
        )
        span *= 2
    return held


def body(
    density,
    space_factor,
    diff_rate,
    loss_inverse,
    chain_yield,
    survival,
    gamma_yield,
    sky_weight,
    sky_blocks,
):
    groups = lax.axis_size("species")
    tiles = lax.axis_size("space")
    rows = NB // tiles

    field = density[0]
    bins = field.shape[0]
    depth = field.shape[3]
    rate = diff_rate[0][:, None, None, None]
    factor = rate * space_factor[None]
    halo = SUBSTEPS
    count = lax.axis_size("space")
    mine = jnp.concatenate([field, space_factor[None]], axis=0)
    from_left = lax.ppermute(
        mine[:, mine.shape[1] - halo:], "space", [(i, i + 1) for i in range(count - 1)]
    )
    from_right = lax.ppermute(mine[:, :halo], "space", [(i + 1, i) for i in range(count - 1)])
    wide = jnp.concatenate([from_left[:bins], field, from_right[:bins]], axis=1)
    wide_factor = rate * jnp.concatenate([from_left[bins], space_factor, from_right[bins]], axis=0)[None]
    for step in range(SUBSTEPS):
        inner = wide[:, 1:-1]
        beside = wide[:, 2:] + wide[:, :-2] + cross_sum(inner)
        wide = inner + wide_factor[:, 1 + step:wide_factor.shape[1] - 1 - step] * (beside - 6.0 * inner)
    field = wide
    solved = jnp.dot(
        loss_inverse[0],
        field.reshape(bins, -1),
        precision=HIGH,
        preferred_element_type=jnp.float32,
    ).reshape(field.shape)
    chain = chain_yield[0]
    own_part = survival[0][:, None, None, None] * solved

    own_columns = jnp.sum(own_part, axis=3).reshape(bins, -1)
    cols = own_columns.shape[1]
    extra = jnp.zeros((2, cols), jnp.float32).at[0, :bins].set(chain).at[1, :bins].set(gamma_yield[0])
    packed = jnp.concatenate([own_columns, extra], axis=0)
    me_g = lax.axis_index("species")
    everyone = packed[None]
    span = 1
    while span < groups:
        other = lax.ppermute(everyone, "species", [(i, i ^ span) for i in range(groups)])
        if span == 1:
            own_part, other = lax.optimization_barrier((own_part, other))
        low = (me_g & span) == 0
        everyone = jnp.where(
            low,
            jnp.concatenate([everyone, other], axis=0),
            jnp.concatenate([other, everyone], axis=0),
        )
        span *= 2
    sums = everyone[0, :bins]
    total = jnp.zeros((cols,), jnp.float32)
    for group in range(groups):
        if group > 0:
            sums = everyone[group, bins, :bins][:, None] * sums + everyone[group, :bins]
        weighted = jnp.dot(
            everyone[group, bins + 1, :bins], sums, precision=HIGH, preferred_element_type=jnp.float32
        )
        emission = lax.reduce_precision(weighted / (bins * depth), exponent_bits=8, mantissa_bits=7)
        total = total + emission
    contribution = jnp.einsum(
        "c,lcb->lb", total, sky_weight[0].astype(jnp.float32), precision=HIGH
    )
    lines, pixels = contribution.shape
    ids = jnp.zeros((1, pixels), jnp.float32).at[0, :lines].set(sky_blocks[0].astype(jnp.float32))
    payload = jnp.concatenate([contribution, ids], axis=0)
    size = bins // CHUNKS
    stack = own_part.reshape((CHUNKS, size) + own_part.shape[1:])
    yields = chain.reshape(CHUNKS, size)[:, :, None, None, None]
    pairs = [(g, g + 1) for g in range(groups - 1)]
    for wave in range(CHUNKS + groups - 2):
        sent = lax.dynamic_index_in_dim(stack, jnp.clip(wave - me_g, 0, CHUNKS - 1), 0, keepdims=False)
        arrived = lax.ppermute(sent, "species", pairs)
        if wave == 0:
            payload, arrived = lax.optimization_barrier((payload, arrived))
        slot = wave - me_g + 1
        valid = (me_g >= 1) & (slot >= 0) & (slot < CHUNKS)
        slot = jnp.clip(slot, 0, CHUNKS - 1)
        current = lax.dynamic_index_in_dim(stack, slot, 0, keepdims=False)
        scale = lax.dynamic_index_in_dim(yields, slot, 0, keepdims=False)
        updated = jnp.where(valid, current + scale * arrived, current)
        stack = lax.dynamic_update_index_in_dim(stack, updated, slot, 0)
    carried = stack.reshape(own_part.shape)
    gathered = gather_all(payload, "space")
    mine = lax.axis_index("space") * rows + jnp.arange(rows, dtype=jnp.int32)
    onehot = (
        gathered[:, lines, :lines].reshape(1, tiles * lines) == mine.astype(jnp.float32)[:, None]
    ).astype(jnp.float32)
    sky = jnp.dot(
        onehot,
        gathered[:, :lines].reshape(tiles * lines, pixels),
        precision=HIGH,
        preferred_element_type=jnp.float32,
    )

    return (carried[None], sky)


def solution(mesh):
    placed = (
        P("species", None, "space", None, None),
        P("space", None, None),
        P("species", None),
        P("species", None, None),
        P("species", None),
        P("species", None),
        P("species", None),
        P("space", None, None, None),
        P("space", None),
    )
    return jax.shard_map(
        body,
        mesh=mesh,
        in_specs=placed,
        out_specs=(P("species", None, "space", None, None), P("space", None)),
        check_vma=False,
    )
```

```python
import jax
import jax.numpy as jnp
from jax import lax
from jax.sharding import PartitionSpec as P

SUBSTEPS = 2
NB = 384
CHUNKS = 4
HIGH = lax.Precision.HIGHEST


def padded_2(cells, sides, width):
    for axis, dim in sides:
        count = lax.axis_size(axis)
        ends = count - 1
        head = lax.slice_in_dim(cells, 0, width, axis=dim)
        tail = lax.slice_in_dim(cells, cells.shape[dim] - width, cells.shape[dim], axis=dim)
        cells = jnp.concatenate(
            [
                lax.ppermute(tail, axis, [(i, (i + 1) % count) for i in range(ends)]),
                cells,
                lax.ppermute(head, axis, [((i + 1) % count, i) for i in range(ends)]),
            ],
            axis=dim,
        )
    return cells


def cross_sum(field):
    padded = jnp.pad(field, ((0, 0), (0, 0), (1, 1), (1, 1)))
    beside = padded[:, :, 2:, 1:-1] + padded[:, :, :-2, 1:-1]
    beside = beside + padded[:, :, 1:-1, 2:] + padded[:, :, 1:-1, :-2]
    return beside


def gather_all(block, axis):
    count = lax.axis_size(axis)
    if count & (count - 1):
        return lax.all_gather(block, axis)
    me = lax.axis_index(axis)
    held = block[None]
    span = 1
    while span < count:
        other = lax.ppermute(held, axis, [(i, i ^ span) for i in range(count)])
        low = (me & span) == 0
        held = jnp.where(
            low,
            jnp.concatenate([held, other], axis=0),
            jnp.concatenate([other, held], axis=0),
        )
        span *= 2
    return held


def body(
    density,
    space_factor,
    diff_rate,
    loss_inverse,
    chain_yield,
    survival,
    gamma_yield,
    sky_weight,
    sky_blocks,
):
    groups = lax.axis_size("species")
    tiles = lax.axis_size("space")
    rows = NB // tiles

    field = density[0]
    bins = field.shape[0]
    depth = field.shape[3]
    rate = diff_rate[0][:, None, None, None]
    factor = rate * space_factor[None]
    halo = SUBSTEPS
    count = lax.axis_size("space")
    mine = jnp.concatenate([field, space_factor[None]], axis=0)
    from_left = lax.ppermute(
        mine[:, mine.shape[1] - halo:], "space", [(i, i + 1) for i in range(count - 1)]
    )
    from_right = lax.ppermute(mine[:, :halo], "space", [(i + 1, i) for i in range(count - 1)])
    wide = jnp.concatenate([from_left[:bins], field, from_right[:bins]], axis=1)
    wide_factor = rate * jnp.concatenate([from_left[bins], space_factor, from_right[bins]], axis=0)[None]
    for step in range(SUBSTEPS):
        inner = wide[:, 1:-1]
        beside = wide[:, 2:] + wide[:, :-2] + cross_sum(inner)
        wide = inner + wide_factor[:, 1 + step:wide_factor.shape[1] - 1 - step] * (beside - 6.0 * inner)
    field = wide
    solved = jnp.dot(
        loss_inverse[0],
        field.reshape(bins, -1),
        precision=HIGH,
        preferred_element_type=jnp.float32,
    ).reshape(field.shape)
    chain = chain_yield[0]
    own_part = survival[0][:, None, None, None] * solved

    own_columns = jnp.sum(own_part, axis=3).reshape(bins, -1)
    cols = own_columns.shape[1]
    extra = jnp.zeros((2, cols), jnp.float32).at[0, :bins].set(chain).at[1, :bins].set(gamma_yield[0])
    packed = jnp.concatenate([own_columns, extra], axis=0)
    me_chain = lax.axis_index("species")
    size = bins // CHUNKS
    stack = own_part.reshape((CHUNKS, size) + own_part.shape[1:])
    yields = chain.reshape(CHUNKS, size)[:, :, None, None, None]
    pairs = [(g, g + 1) for g in range(groups - 1)]
    for wave in range(CHUNKS + groups - 2):
        sent = lax.dynamic_index_in_dim(stack, jnp.clip(wave - me_chain, 0, CHUNKS - 1), 0, keepdims=False)
        arrived = lax.ppermute(sent, "species", pairs)
        if wave == 0:
            packed, arrived = lax.optimization_barrier((packed, arrived))
        slot = wave - me_chain + 1
        valid = (me_chain >= 1) & (slot >= 0) & (slot < CHUNKS)
        slot = jnp.clip(slot, 0, CHUNKS - 1)
        current = lax.dynamic_index_in_dim(stack, slot, 0, keepdims=False)
        scale = lax.dynamic_index_in_dim(yields, slot, 0, keepdims=False)
        updated = jnp.where(valid, current + scale * arrived, current)
        stack = lax.dynamic_update_index_in_dim(stack, updated, slot, 0)
    carried = stack.reshape(own_part.shape)
    me_g = lax.axis_index("species")
    everyone = packed[None]
    span = 1
    while span < groups:
        other = lax.ppermute(everyone, "species", [(i, i ^ span) for i in range(groups)])
        low = (me_g & span) == 0
        everyone = jnp.where(
            low,
            jnp.concatenate([everyone, other], axis=0),
            jnp.concatenate([other, everyone], axis=0),
        )
        span *= 2
    sums = everyone[0, :bins]
    total = jnp.zeros((cols,), jnp.float32)
    for group in range(groups):
        if group > 0:
            sums = everyone[group, bins, :bins][:, None] * sums + everyone[group, :bins]
        weighted = jnp.dot(
            everyone[group, bins + 1, :bins], sums, precision=HIGH, preferred_element_type=jnp.float32
        )
        emission = lax.reduce_precision(weighted / (bins * depth), exponent_bits=8, mantissa_bits=7)
        total = total + emission
    contribution = jnp.einsum(
        "c,lcb->lb", total, sky_weight[0].astype(jnp.float32), precision=HIGH
    )
    lines, pixels = contribution.shape
    ids = jnp.zeros((1, pixels), jnp.float32).at[0, :lines].set(sky_blocks[0].astype(jnp.float32))
    payload = jnp.concatenate([contribution, ids], axis=0)
    gathered = gather_all(payload, "space")
    mine = lax.axis_index("space") * rows + jnp.arange(rows, dtype=jnp.int32)
    onehot = (
        gathered[:, lines, :lines].reshape(1, tiles * lines) == mine.astype(jnp.float32)[:, None]
    ).astype(jnp.float32)
    sky = jnp.dot(
        onehot,
        gathered[:, :lines].reshape(tiles * lines, pixels),
        precision=HIGH,
        preferred_element_type=jnp.float32,
    )

    return (carried[None], sky)


def solution(mesh):
    placed = (
        P("species", None, "space", None, None),
        P("space", None, None),
        P("species", None),
        P("species", None, None),
        P("species", None),
        P("species", None),
        P("species", None),
        P("space", None, None, None),
        P("space", None),
    )
    return jax.shard_map(
        body,
        mesh=mesh,
        in_specs=placed,
        out_specs=(P("species", None, "space", None, None), P("space", None)),
        check_vma=False,
    )
```

```python
import jax
import jax.numpy as jnp
from jax import lax
from jax.sharding import PartitionSpec as P

SUBSTEPS = 2
NB = 384
CHUNKS = 4
HIGH = lax.Precision.HIGHEST


def padded_2(cells, sides, width):
    for axis, dim in sides:
        count = lax.axis_size(axis)
        ends = count - 1
        head = lax.slice_in_dim(cells, 0, width, axis=dim)
        tail = lax.slice_in_dim(cells, cells.shape[dim] - width, cells.shape[dim], axis=dim)
        cells = jnp.concatenate(
            [
                lax.ppermute(tail, axis, [(i, (i + 1) % count) for i in range(ends)]),
                cells,
                lax.ppermute(head, axis, [((i + 1) % count, i) for i in range(ends)]),
            ],
            axis=dim,
        )
    return cells


def cross_sum(field):
    padded = jnp.pad(field, ((0, 0), (0, 0), (1, 1), (1, 1)))
    beside = padded[:, :, 2:, 1:-1] + padded[:, :, :-2, 1:-1]
    beside = beside + padded[:, :, 1:-1, 2:] + padded[:, :, 1:-1, :-2]
    return beside


def gather_all(block, axis):
    count = lax.axis_size(axis)
    if count & (count - 1):
        return lax.all_gather(block, axis)
    me = lax.axis_index(axis)
    held = block[None]
    span = 1
    while span < count:
        other = lax.ppermute(held, axis, [(i, i ^ span) for i in range(count)])
        low = (me & span) == 0
        held = jnp.where(
            low,
            jnp.concatenate([held, other], axis=0),
            jnp.concatenate([other, held], axis=0),
        )
        span *= 2
    return held


def body(
    density,
    space_factor,
    diff_rate,
    loss_inverse,
    chain_yield,
    survival,
    gamma_yield,
    sky_weight,
    sky_blocks,
):
    groups = lax.axis_size("species")
    tiles = lax.axis_size("space")
    rows = NB // tiles

    field = density[0]
    bins = field.shape[0]
    depth = field.shape[3]
    rate = diff_rate[0][:, None, None, None]
    factor = rate * space_factor[None]
    halo = SUBSTEPS
    count = lax.axis_size("space")
    mine = jnp.concatenate([field, space_factor[None]], axis=0)
    from_left = lax.ppermute(
        mine[:, mine.shape[1] - halo:], "space", [(i, i + 1) for i in range(count - 1)]
    )
    from_right = lax.ppermute(mine[:, :halo], "space", [(i + 1, i) for i in range(count - 1)])
    wide = jnp.concatenate([from_left[:bins], field, from_right[:bins]], axis=1)
    wide_factor = rate * jnp.concatenate([from_left[bins], space_factor, from_right[bins]], axis=0)[None]
    for step in range(SUBSTEPS):
        inner = wide[:, 1:-1]
        beside = wide[:, 2:] + wide[:, :-2] + cross_sum(inner)
        wide = inner + wide_factor[:, 1 + step:wide_factor.shape[1] - 1 - step] * (beside - 6.0 * inner)
    field = wide
    solved = jnp.dot(
        loss_inverse[0],
        field.reshape(bins, -1),
        precision=HIGH,
        preferred_element_type=jnp.float32,
    ).reshape(field.shape)
    chain = chain_yield[0]
    own_part = survival[0][:, None, None, None] * solved

    own_columns = jnp.sum(own_part, axis=3).reshape(bins, -1)
    cols = own_columns.shape[1]
    extra = jnp.zeros((2, cols), jnp.float32).at[0, :bins].set(chain).at[1, :bins].set(gamma_yield[0])
    packed = jnp.concatenate([own_columns, extra], axis=0)
    me_chain = lax.axis_index("species")
    size = bins // CHUNKS
    stack = own_part.reshape((CHUNKS, size) + own_part.shape[1:])
    yields = chain.reshape(CHUNKS, size)[:, :, None, None, None]
    pairs = [(g, g + 1) for g in range(groups - 1)]
    for wave in range(CHUNKS + groups - 2):
        sent = lax.dynamic_index_in_dim(stack, jnp.clip(wave - me_chain, 0, CHUNKS - 1), 0, keepdims=False)
        arrived = lax.ppermute(sent, "species", pairs)
        if wave == 0:
            packed, arrived = lax.optimization_barrier((packed, arrived))
        slot = wave - me_chain + 1
        valid = (me_chain >= 1) & (slot >= 0) & (slot < CHUNKS)
        slot = jnp.clip(slot, 0, CHUNKS - 1)
        current = lax.dynamic_index_in_dim(stack, slot, 0, keepdims=False)
        scale = lax.dynamic_index_in_dim(yields, slot, 0, keepdims=False)
        updated = jnp.where(valid, current + scale * arrived, current)
        stack = lax.dynamic_update_index_in_dim(stack, updated, slot, 0)
    carried = stack.reshape(own_part.shape)
    me_g = lax.axis_index("species")
    everyone = packed[None]
    span = 1
    while span < groups:
        other = lax.ppermute(everyone, "species", [(i, i ^ span) for i in range(groups)])
        low = (me_g & span) == 0
        everyone = jnp.where(
            low,
            jnp.concatenate([everyone, other], axis=0),
            jnp.concatenate([other, everyone], axis=0),
        )
        span *= 2
    sums = everyone[0, :bins]
    total = jnp.zeros((cols,), jnp.float32)
    for group in range(groups):
        if group > 0:
            sums = everyone[group, bins, :bins][:, None] * sums + everyone[group, :bins]
        weighted = jnp.dot(
            everyone[group, bins + 1, :bins], sums, precision=HIGH, preferred_element_type=jnp.float32
        )
        emission = lax.reduce_precision(weighted / (bins * depth), exponent_bits=8, mantissa_bits=7)
        total = total + emission
    contribution = jnp.einsum(
        "c,lcb->lb", total, sky_weight[0].astype(jnp.float32), precision=HIGH
    )
    lines, pixels = contribution.shape
    ids = jnp.zeros((1, pixels), jnp.float32).at[0, :lines].set(sky_blocks[0].astype(jnp.float32))
    payload = jnp.concatenate([contribution, ids], axis=0)
    big = jnp.zeros((256, payload.shape[1]), jnp.float32).at[:payload.shape[0]].set(payload)
    gathered = lax.all_gather(big, "space")[:, :payload.shape[0]]
    mine = lax.axis_index("space") * rows + jnp.arange(rows, dtype=jnp.int32)
    onehot = (
        gathered[:, lines, :lines].reshape(1, tiles * lines) == mine.astype(jnp.float32)[:, None]
    ).astype(jnp.float32)
    sky = jnp.dot(
        onehot,
        gathered[:, :lines].reshape(tiles * lines, pixels),
        precision=HIGH,
        preferred_element_type=jnp.float32,
    )

    return (carried[None], sky)


def solution(mesh):
    placed = (
        P("species", None, "space", None, None),
        P("space", None, None),
        P("species", None),
        P("species", None, None),
        P("species", None),
        P("species", None),
        P("species", None),
        P("space", None, None, None),
        P("space", None),
    )
    return jax.shard_map(
        body,
        mesh=mesh,
        in_specs=placed,
        out_specs=(P("species", None, "space", None, None), P("space", None)),
        check_vma=False,
    )
```

```python
import jax
import jax.numpy as jnp
from jax import lax
from jax.sharding import PartitionSpec as P

SUBSTEPS = 2
NB = 384
CHUNKS = 4
HIGH = lax.Precision.HIGHEST


def padded_2(cells, sides, width):
    for axis, dim in sides:
        count = lax.axis_size(axis)
        ends = count - 1
        head = lax.slice_in_dim(cells, 0, width, axis=dim)
        tail = lax.slice_in_dim(cells, cells.shape[dim] - width, cells.shape[dim], axis=dim)
        cells = jnp.concatenate(
            [
                lax.ppermute(tail, axis, [(i, (i + 1) % count) for i in range(ends)]),
                cells,
                lax.ppermute(head, axis, [((i + 1) % count, i) for i in range(ends)]),
            ],
            axis=dim,
        )
    return cells


def cross_sum(field):
    padded = jnp.pad(field, ((0, 0), (0, 0), (1, 1), (1, 1)))
    beside = padded[:, :, 2:, 1:-1] + padded[:, :, :-2, 1:-1]
    beside = beside + padded[:, :, 1:-1, 2:] + padded[:, :, 1:-1, :-2]
    return beside


def gather_all(block, axis):
    count = lax.axis_size(axis)
    me = lax.axis_index(axis)
    by_shift = [block] + [
        lax.ppermute(block, axis, [(i, (i + d) % count) for i in range(count)])
        for d in range(1, count)
    ]
    stacked = jnp.stack(by_shift)
    order = (me - jnp.arange(count)) % count
    return jnp.take(stacked, order, axis=0)


def body(
    density,
    space_factor,
    diff_rate,
    loss_inverse,
    chain_yield,
    survival,
    gamma_yield,
    sky_weight,
    sky_blocks,
):
    groups = lax.axis_size("species")
    tiles = lax.axis_size("space")
    rows = NB // tiles

    field = density[0]
    bins = field.shape[0]
    depth = field.shape[3]
    rate = diff_rate[0][:, None, None, None]
    factor = rate * space_factor[None]
    halo = SUBSTEPS
    count = lax.axis_size("space")
    mine = jnp.concatenate([field, space_factor[None]], axis=0)
    from_left = lax.ppermute(
        mine[:, mine.shape[1] - halo:], "space", [(i, i + 1) for i in range(count - 1)]
    )
    from_right = lax.ppermute(mine[:, :halo], "space", [(i + 1, i) for i in range(count - 1)])
    wide = jnp.concatenate([from_left[:bins], field, from_right[:bins]], axis=1)
    wide_factor = rate * jnp.concatenate([from_left[bins], space_factor, from_right[bins]], axis=0)[None]
    for step in range(SUBSTEPS):
        inner = wide[:, 1:-1]
        beside = wide[:, 2:] + wide[:, :-2] + cross_sum(inner)
        wide = inner + wide_factor[:, 1 + step:wide_factor.shape[1] - 1 - step] * (beside - 6.0 * inner)
    field = wide
    solved = jnp.dot(
        loss_inverse[0],
        field.reshape(bins, -1),
        precision=HIGH,
        preferred_element_type=jnp.float32,
    ).reshape(field.shape)
    chain = chain_yield[0]
    own_part = survival[0][:, None, None, None] * solved

    own_columns = jnp.sum(own_part, axis=3).reshape(bins, -1)
    cols = own_columns.shape[1]
    extra = jnp.zeros((2, cols), jnp.float32).at[0, :bins].set(chain).at[1, :bins].set(gamma_yield[0])
    packed = jnp.concatenate([own_columns, extra], axis=0)
    everyone = gather_all(packed, "species")
    sums = everyone[0, :bins]
    total = jnp.zeros((cols,), jnp.float32)
    for group in range(groups):
        if group > 0:
            sums = everyone[group, bins, :bins][:, None] * sums + everyone[group, :bins]
        weighted = jnp.dot(
            everyone[group, bins + 1, :bins], sums, precision=HIGH, preferred_element_type=jnp.float32
        )
        emission = lax.reduce_precision(weighted / (bins * depth), exponent_bits=8, mantissa_bits=7)
        total = total + emission
    contribution = jnp.einsum(
        "c,lcb->lb", total, sky_weight[0].astype(jnp.float32), precision=HIGH
    )
    lines, pixels = contribution.shape
    ids = jnp.zeros((1, pixels), jnp.float32).at[0, :lines].set(sky_blocks[0].astype(jnp.float32))
    payload = jnp.concatenate([contribution, ids], axis=0)
    base = bins // CHUNKS
    bounds = [0]
    for c in range(CHUNKS):
        bounds.append(bounds[-1] + base + 2 * c - (CHUNKS - 1))
    bounds[-1] = bins
    pieces = [own_part[bounds[c]:bounds[c + 1]] for c in range(CHUNKS)]
    scales = [chain[bounds[c]:bounds[c + 1]][:, None, None, None] for c in range(CHUNKS)]
    for wave in range(CHUNKS + groups - 2):
        for c in range(CHUNKS):
            s = wave - c
            if 0 <= s < groups - 1:
                arrived = lax.ppermute(pieces[c], "species", [(s, s + 1)])
                if s == 0 and c == CHUNKS - 1:
                    payload, arrived = lax.optimization_barrier((payload, arrived))
                pieces[c] = pieces[c] + scales[c] * arrived
    carried = jnp.concatenate(pieces, axis=0)
    gathered = gather_all(payload, "space")
    mine = lax.axis_index("space") * rows + jnp.arange(rows, dtype=jnp.int32)
    onehot = (
        gathered[:, lines, :lines].reshape(1, tiles * lines) == mine.astype(jnp.float32)[:, None]
    ).astype(jnp.float32)
    sky = jnp.dot(
        onehot,
        gathered[:, :lines].reshape(tiles * lines, pixels),
        precision=HIGH,
        preferred_element_type=jnp.float32,
    )

    return (carried[None], sky)


def solution(mesh):
    placed = (
        P("species", None, "space", None, None),
        P("space", None, None),
        P("species", None),
        P("species", None, None),
        P("species", None),
        P("species", None),
        P("species", None),
        P("space", None, None, None),
        P("space", None),
    )
    return jax.shard_map(
        body,
        mesh=mesh,
        in_specs=placed,
        out_specs=(P("species", None, "space", None, None), P("space", None)),
        check_vma=False,
    )
```

```python
import jax
import jax.numpy as jnp
from jax import lax
from jax.sharding import PartitionSpec as P

SUBSTEPS = 2
NB = 384
CHUNKS = 4
HIGH = lax.Precision.HIGHEST


def padded_2(cells, sides, width):
    for axis, dim in sides:
        count = lax.axis_size(axis)
        ends = count - 1
        head = lax.slice_in_dim(cells, 0, width, axis=dim)
        tail = lax.slice_in_dim(cells, cells.shape[dim] - width, cells.shape[dim], axis=dim)
        cells = jnp.concatenate(
            [
                lax.ppermute(tail, axis, [(i, (i + 1) % count) for i in range(ends)]),
                cells,
                lax.ppermute(head, axis, [((i + 1) % count, i) for i in range(ends)]),
            ],
            axis=dim,
        )
    return cells


def cross_sum(field):
    padded = jnp.pad(field, ((0, 0), (0, 0), (1, 1), (1, 1)))
    beside = padded[:, :, 2:, 1:-1] + padded[:, :, :-2, 1:-1]
    beside = beside + padded[:, :, 1:-1, 2:] + padded[:, :, 1:-1, :-2]
    return beside


def gather_all(block, axis):
    count = lax.axis_size(axis)
    if count & (count - 1):
        return lax.all_gather(block, axis)
    me = lax.axis_index(axis)
    held = block[None]
    span = 1
    while span < count:
        other = lax.ppermute(held, axis, [(i, i ^ span) for i in range(count)])
        low = (me & span) == 0
        held = jnp.where(
            low,
            jnp.concatenate([held, other], axis=0),
            jnp.concatenate([other, held], axis=0),
        )
        span *= 2
    return held


def body(
    density,
    space_factor,
    diff_rate,
    loss_inverse,
    chain_yield,
    survival,
    gamma_yield,
    sky_weight,
    sky_blocks,
):
    groups = lax.axis_size("species")
    tiles = lax.axis_size("space")
    rows = NB // tiles

    field = density[0]
    bins = field.shape[0]
    depth = field.shape[3]
    rate = diff_rate[0][:, None, None, None]
    factor = rate * space_factor[None]
    halo = SUBSTEPS
    count = lax.axis_size("space")
    mine = jnp.concatenate([field, space_factor[None]], axis=0)
    from_left = lax.ppermute(
        mine[:, mine.shape[1] - halo:], "space", [(i, i + 1) for i in range(count - 1)]
    )
    from_right = lax.ppermute(mine[:, :halo], "space", [(i + 1, i) for i in range(count - 1)])
    wide = jnp.concatenate([from_left[:bins], field, from_right[:bins]], axis=1)
    wide_factor = rate * jnp.concatenate([from_left[bins], space_factor, from_right[bins]], axis=0)[None]
    for step in range(SUBSTEPS):
        inner = wide[:, 1:-1]
        beside = wide[:, 2:] + wide[:, :-2] + cross_sum(inner)
        wide = inner + wide_factor[:, 1 + step:wide_factor.shape[1] - 1 - step] * (beside - 6.0 * inner)
    field = wide
    solved = jnp.dot(
        loss_inverse[0],
        field.reshape(bins, -1),
        precision=HIGH,
        preferred_element_type=jnp.float32,
    ).reshape(field.shape)
    chain = chain_yield[0]
    own_part = survival[0][:, None, None, None] * solved

    own_columns = jnp.sum(own_part, axis=3).reshape(bins, -1)
    cols = own_columns.shape[1]
    extra = jnp.zeros((2, cols), jnp.float32).at[0, :bins].set(chain).at[1, :bins].set(gamma_yield[0])
    packed = jnp.concatenate([own_columns, extra], axis=0)
    base = bins // CHUNKS
    bounds = [0]
    for c in range(CHUNKS):
        bounds.append(bounds[-1] + base + 2 * c - (CHUNKS - 1))
    bounds[-1] = bins
    pieces = [own_part[bounds[c]:bounds[c + 1]] for c in range(CHUNKS)]
    scales = [chain[bounds[c]:bounds[c + 1]][:, None, None, None] for c in range(CHUNKS)]
    for wave in range(CHUNKS + groups - 2):
        for c in range(CHUNKS):
            s = wave - c
            if 0 <= s < groups - 1:
                arrived = lax.ppermute(pieces[c], "species", [(s, s + 1)])
                pieces[c] = pieces[c] + scales[c] * arrived
    packed, pieces = lax.optimization_barrier((packed, pieces))
    carried = jnp.concatenate(pieces, axis=0)
    me_g = lax.axis_index("species")
    everyone = packed[None]
    span = 1
    while span < groups:
        other = lax.ppermute(everyone, "species", [(i, i ^ span) for i in range(groups)])
        low = (me_g & span) == 0
        everyone = jnp.where(
            low,
            jnp.concatenate([everyone, other], axis=0),
            jnp.concatenate([other, everyone], axis=0),
        )
        span *= 2
    sums = everyone[0, :bins]
    total = jnp.zeros((cols,), jnp.float32)
    for group in range(groups):
        if group > 0:
            sums = everyone[group, bins, :bins][:, None] * sums + everyone[group, :bins]
        weighted = jnp.dot(
            everyone[group, bins + 1, :bins], sums, precision=HIGH, preferred_element_type=jnp.float32
        )
        emission = lax.reduce_precision(weighted / (bins * depth), exponent_bits=8, mantissa_bits=7)
        total = total + emission
    contribution = jnp.einsum(
        "c,lcb->lb", total, sky_weight[0].astype(jnp.float32), precision=HIGH
    )
    lines, pixels = contribution.shape
    ids = jnp.zeros((1, pixels), jnp.float32).at[0, :lines].set(sky_blocks[0].astype(jnp.float32))
    payload = jnp.concatenate([contribution, ids], axis=0)
    gathered = gather_all(payload, "space")
    mine = lax.axis_index("space") * rows + jnp.arange(rows, dtype=jnp.int32)
    onehot = (
        gathered[:, lines, :lines].reshape(1, tiles * lines) == mine.astype(jnp.float32)[:, None]
    ).astype(jnp.float32)
    sky = jnp.dot(
        onehot,
        gathered[:, :lines].reshape(tiles * lines, pixels),
        precision=HIGH,
        preferred_element_type=jnp.float32,
    )

    return (carried[None], sky)


def solution(mesh):
    placed = (
        P("species", None, "space", None, None),
        P("space", None, None),
        P("species", None),
        P("species", None, None),
        P("species", None),
        P("species", None),
        P("species", None),
        P("space", None, None, None),
        P("space", None),
    )
    return jax.shard_map(
        body,
        mesh=mesh,
        in_specs=placed,
        out_specs=(P("species", None, "space", None, None), P("space", None)),
        check_vma=False,
    )
```

```python
import jax
import jax.numpy as jnp
from jax import lax
from jax.sharding import PartitionSpec as P

SUBSTEPS = 2
NB = 384
CHUNKS = 4
HIGH = lax.Precision.HIGHEST


def padded_2(cells, sides, width):
    for axis, dim in sides:
        count = lax.axis_size(axis)
        ends = count - 1
        head = lax.slice_in_dim(cells, 0, width, axis=dim)
        tail = lax.slice_in_dim(cells, cells.shape[dim] - width, cells.shape[dim], axis=dim)
        cells = jnp.concatenate(
            [
                lax.ppermute(tail, axis, [(i, (i + 1) % count) for i in range(ends)]),
                cells,
                lax.ppermute(head, axis, [((i + 1) % count, i) for i in range(ends)]),
            ],
            axis=dim,
        )
    return cells


def cross_sum(field):
    padded = jnp.pad(field, ((0, 0), (0, 0), (1, 1), (1, 1)))
    beside = padded[:, :, 2:, 1:-1] + padded[:, :, :-2, 1:-1]
    beside = beside + padded[:, :, 1:-1, 2:] + padded[:, :, 1:-1, :-2]
    return beside


def gather_all(block, axis):
    count = lax.axis_size(axis)
    if count & (count - 1):
        return lax.all_gather(block, axis)
    me = lax.axis_index(axis)
    held = block[None]
    span = 1
    while span < count:
        other = lax.ppermute(held, axis, [(i, i ^ span) for i in range(count)])
        low = (me & span) == 0
        held = jnp.where(
            low,
            jnp.concatenate([held, other], axis=0),
            jnp.concatenate([other, held], axis=0),
        )
        span *= 2
    return held


def body(
    density,
    space_factor,
    diff_rate,
    loss_inverse,
    chain_yield,
    survival,
    gamma_yield,
    sky_weight,
    sky_blocks,
):
    groups = lax.axis_size("species")
    tiles = lax.axis_size("space")
    rows = NB // tiles

    field = density[0]
    bins = field.shape[0]
    depth = field.shape[3]
    rate = diff_rate[0][:, None, None, None]
    factor = rate * space_factor[None]
    halo = SUBSTEPS
    count = lax.axis_size("space")
    mine = jnp.concatenate([field, space_factor[None]], axis=0)
    from_left = lax.ppermute(
        mine[:, mine.shape[1] - halo:], "space", [(i, i + 1) for i in range(count - 1)]
    )
    from_right = lax.ppermute(mine[:, :halo], "space", [(i + 1, i) for i in range(count - 1)])
    wide = jnp.concatenate([from_left[:bins], field, from_right[:bins]], axis=1)
    wide_factor = rate * jnp.concatenate([from_left[bins], space_factor, from_right[bins]], axis=0)[None]
    for step in range(SUBSTEPS):
        inner = wide[:, 1:-1]
        beside = wide[:, 2:] + wide[:, :-2] + cross_sum(inner)
        wide = inner + wide_factor[:, 1 + step:wide_factor.shape[1] - 1 - step] * (beside - 6.0 * inner)
    field = wide
    solved = jnp.dot(
        loss_inverse[0],
        field.reshape(bins, -1),
        precision=HIGH,
        preferred_element_type=jnp.float32,
    ).reshape(field.shape)
    chain = chain_yield[0]
    own_part = survival[0][:, None, None, None] * solved

    own_columns = jnp.sum(own_part, axis=3).reshape(bins, -1)
    cols = own_columns.shape[1]
    extra = jnp.zeros((2, cols), jnp.float32).at[0, :bins].set(chain).at[1, :bins].set(gamma_yield[0])
    packed = jnp.concatenate([own_columns, extra], axis=0)
    me_g = lax.axis_index("species")
    everyone = packed[None]
    span = 1
    while span < groups:
        other = lax.ppermute(everyone, "species", [(i, i ^ span) for i in range(groups)])
        if span == 1:
            own_part, other = lax.optimization_barrier((own_part, other))
        low = (me_g & span) == 0
        everyone = jnp.where(
            low,
            jnp.concatenate([everyone, other], axis=0),
            jnp.concatenate([other, everyone], axis=0),
        )
        span *= 2
    sums = everyone[0, :bins]
    total = jnp.zeros((cols,), jnp.float32)
    for group in range(groups):
        if group > 0:
            sums = everyone[group, bins, :bins][:, None] * sums + everyone[group, :bins]
        weighted = jnp.dot(
            everyone[group, bins + 1, :bins], sums, precision=HIGH, preferred_element_type=jnp.float32
        )
        emission = lax.reduce_precision(weighted / (bins * depth), exponent_bits=8, mantissa_bits=7)
        total = total + emission
    contribution = jnp.einsum(
        "c,lcb->lb", total, sky_weight[0].astype(jnp.float32), precision=HIGH
    )
    lines, pixels = contribution.shape
    ids = jnp.zeros((1, pixels), jnp.float32).at[0, :lines].set(sky_blocks[0].astype(jnp.float32))
    payload = jnp.concatenate([contribution, ids], axis=0)
    slabs = own_part.reshape((bins, own_part.shape[1], groups, -1) + own_part.shape[3:])
    slabs = jnp.moveaxis(slabs, 2, 0)
    me_s = lax.axis_index("species")
    shifts = list(range(1, groups))
    by_shift = [lax.dynamic_index_in_dim(slabs, me_s, 0, keepdims=False)]
    for d in shifts:
        outgoing = lax.dynamic_index_in_dim(slabs, (me_s + d) % groups, 0, keepdims=False)
        by_shift.append(lax.ppermute(outgoing, "species", [(i, (i + d) % groups) for i in range(groups)]))
    parts = jnp.take(jnp.stack(by_shift), (me_s - jnp.arange(groups)) % groups, axis=0)
    running = parts[0]
    results = [running]
    for group in range(1, groups):
        running = everyone[group, bins, :bins][:, None, None, None] * running + parts[group]
        results.append(running)
    results = jnp.stack(results)
    back = [lax.dynamic_index_in_dim(results, me_s, 0, keepdims=False)]
    for d in shifts:
        outgoing = lax.dynamic_index_in_dim(results, (me_s + d) % groups, 0, keepdims=False)
        back.append(lax.ppermute(outgoing, "species", [(i, (i + d) % groups) for i in range(groups)]))
    mine_slabs = jnp.take(jnp.stack(back), (me_s - jnp.arange(groups)) % groups, axis=0)
    carried = jnp.moveaxis(mine_slabs, 0, 2).reshape(own_part.shape)
    gathered = gather_all(payload, "space")
    mine = lax.axis_index("space") * rows + jnp.arange(rows, dtype=jnp.int32)
    onehot = (
        gathered[:, lines, :lines].reshape(1, tiles * lines) == mine.astype(jnp.float32)[:, None]
    ).astype(jnp.float32)
    sky = jnp.dot(
        onehot,
        gathered[:, :lines].reshape(tiles * lines, pixels),
        precision=HIGH,
        preferred_element_type=jnp.float32,
    )

    return (carried[None], sky)


def solution(mesh):
    placed = (
        P("species", None, "space", None, None),
        P("space", None, None),
        P("species", None),
        P("species", None, None),
        P("species", None),
        P("species", None),
        P("species", None),
        P("space", None, None, None),
        P("space", None),
    )
    return jax.shard_map(
        body,
        mesh=mesh,
        in_specs=placed,
        out_specs=(P("species", None, "space", None, None), P("space", None)),
        check_vma=False,
    )
```

```python
import jax
import jax.numpy as jnp
from jax import lax
from jax.sharding import PartitionSpec as P

SUBSTEPS = 2
NB = 384
CHUNKS = 4
HIGH = lax.Precision.HIGHEST


def padded_2(cells, sides, width):
    for axis, dim in sides:
        count = lax.axis_size(axis)
        ends = count - 1
        head = lax.slice_in_dim(cells, 0, width, axis=dim)
        tail = lax.slice_in_dim(cells, cells.shape[dim] - width, cells.shape[dim], axis=dim)
        cells = jnp.concatenate(
            [
                lax.ppermute(tail, axis, [(i, (i + 1) % count) for i in range(ends)]),
                cells,
                lax.ppermute(head, axis, [((i + 1) % count, i) for i in range(ends)]),
            ],
            axis=dim,
        )
    return cells


def cross_sum(field):
    padded = jnp.pad(field, ((0, 0), (0, 0), (1, 1), (1, 1)))
    beside = padded[:, :, 2:, 1:-1] + padded[:, :, :-2, 1:-1]
    beside = beside + padded[:, :, 1:-1, 2:] + padded[:, :, 1:-1, :-2]
    return beside


def gather_all(block, axis):
    count = lax.axis_size(axis)
    if count & (count - 1):
        return lax.all_gather(block, axis)
    me = lax.axis_index(axis)
    held = block[None]
    span = 1
    while span < count:
        other = lax.ppermute(held, axis, [(i, i ^ span) for i in range(count)])
        low = (me & span) == 0
        held = jnp.where(
            low,
            jnp.concatenate([held, other], axis=0),
            jnp.concatenate([other, held], axis=0),
        )
        span *= 2
    return held


def body(
    density,
    space_factor,
    diff_rate,
    loss_inverse,
    chain_yield,
    survival,
    gamma_yield,
    sky_weight,
    sky_blocks,
):
    groups = lax.axis_size("species")
    tiles = lax.axis_size("space")
    rows = NB // tiles

    yields_all = gather_all(chain_yield[0], "species")
    field = density[0]
    bins = field.shape[0]
    depth = field.shape[3]
    rate = diff_rate[0][:, None, None, None]
    factor = rate * space_factor[None]
    halo = SUBSTEPS
    count = lax.axis_size("space")
    mine = jnp.concatenate([field, space_factor[None]], axis=0)
    from_left = lax.ppermute(
        mine[:, mine.shape[1] - halo:], "space", [(i, i + 1) for i in range(count - 1)]
    )
    from_right = lax.ppermute(mine[:, :halo], "space", [(i + 1, i) for i in range(count - 1)])
    wide = jnp.concatenate([from_left[:bins], field, from_right[:bins]], axis=1)
    wide_factor = rate * jnp.concatenate([from_left[bins], space_factor, from_right[bins]], axis=0)[None]
    for step in range(SUBSTEPS):
        inner = wide[:, 1:-1]
        beside = wide[:, 2:] + wide[:, :-2] + cross_sum(inner)
        wide = inner + wide_factor[:, 1 + step:wide_factor.shape[1] - 1 - step] * (beside - 6.0 * inner)
    field = wide
    solved = jnp.dot(
        loss_inverse[0],
        field.reshape(bins, -1),
        precision=HIGH,
        preferred_element_type=jnp.float32,
    ).reshape(field.shape)
    chain = chain_yield[0]
    own_part = survival[0][:, None, None, None] * solved

    own_columns = jnp.sum(own_part, axis=3).reshape(bins, -1)
    cols = own_columns.shape[1]
    extra = jnp.zeros((2, cols), jnp.float32).at[0, :bins].set(chain).at[1, :bins].set(gamma_yield[0])
    packed = jnp.concatenate([own_columns, extra], axis=0)
    slabs = own_part.reshape((bins, own_part.shape[1], groups, -1) + own_part.shape[3:])
    slabs = jnp.moveaxis(slabs, 2, 0)
    me_s = lax.axis_index("species")
    shifts = list(range(1, groups))
    by_shift = [lax.dynamic_index_in_dim(slabs, me_s, 0, keepdims=False)]
    for d in shifts:
        outgoing = lax.dynamic_index_in_dim(slabs, (me_s + d) % groups, 0, keepdims=False)
        by_shift.append(lax.ppermute(outgoing, "species", [(i, (i + d) % groups) for i in range(groups)]))
    packed, by_shift = lax.optimization_barrier((packed, by_shift))
    parts = jnp.take(jnp.stack(by_shift), (me_s - jnp.arange(groups)) % groups, axis=0)
    me_g = lax.axis_index("species")
    everyone = packed[None]
    span = 1
    while span < groups:
        other = lax.ppermute(everyone, "species", [(i, i ^ span) for i in range(groups)])
        low = (me_g & span) == 0
        everyone = jnp.where(
            low,
            jnp.concatenate([everyone, other], axis=0),
            jnp.concatenate([other, everyone], axis=0),
        )
        span *= 2
    sums = everyone[0, :bins]
    total = jnp.zeros((cols,), jnp.float32)
    for group in range(groups):
        if group > 0:
            sums = everyone[group, bins, :bins][:, None] * sums + everyone[group, :bins]
        weighted = jnp.dot(
            everyone[group, bins + 1, :bins], sums, precision=HIGH, preferred_element_type=jnp.float32
        )
        emission = lax.reduce_precision(weighted / (bins * depth), exponent_bits=8, mantissa_bits=7)
        total = total + emission
    contribution = jnp.einsum(
        "c,lcb->lb", total, sky_weight[0].astype(jnp.float32), precision=HIGH
    )
    lines, pixels = contribution.shape
    ids = jnp.zeros((1, pixels), jnp.float32).at[0, :lines].set(sky_blocks[0].astype(jnp.float32))
    payload = jnp.concatenate([contribution, ids], axis=0)
    running = parts[0]
    results = [running]
    for group in range(1, groups):
        running = yields_all[group][:, None, None, None] * running + parts[group]
        results.append(running)
    results = jnp.stack(results)
    back = [lax.dynamic_index_in_dim(results, me_s, 0, keepdims=False)]
    for d in shifts:
        outgoing = lax.dynamic_index_in_dim(results, (me_s + d) % groups, 0, keepdims=False)
        back.append(lax.ppermute(outgoing, "species", [(i, (i + d) % groups) for i in range(groups)]))
    mine_slabs = jnp.take(jnp.stack(back), (me_s - jnp.arange(groups)) % groups, axis=0)
    carried = jnp.moveaxis(mine_slabs, 0, 2).reshape(own_part.shape)
    gathered = gather_all(payload, "space")
    mine = lax.axis_index("space") * rows + jnp.arange(rows, dtype=jnp.int32)
    onehot = (
        gathered[:, lines, :lines].reshape(1, tiles * lines) == mine.astype(jnp.float32)[:, None]
    ).astype(jnp.float32)
    sky = jnp.dot(
        onehot,
        gathered[:, :lines].reshape(tiles * lines, pixels),
        precision=HIGH,
        preferred_element_type=jnp.float32,
    )

    return (carried[None], sky)


def solution(mesh):
    placed = (
        P("species", None, "space", None, None),
        P("space", None, None),
        P("species", None),
        P("species", None, None),
        P("species", None),
        P("species", None),
        P("species", None),
        P("space", None, None, None),
        P("space", None),
    )
    return jax.shard_map(
        body,
        mesh=mesh,
        in_specs=placed,
        out_specs=(P("species", None, "space", None, None), P("space", None)),
        check_vma=False,
    )
```

```python
import jax
import jax.numpy as jnp
from jax import lax
from jax.sharding import PartitionSpec as P

SUBSTEPS = 2
NB = 384
CHUNKS = 4
HIGH = lax.Precision.HIGHEST


def padded_2(cells, sides, width):
    for axis, dim in sides:
        count = lax.axis_size(axis)
        ends = count - 1
        head = lax.slice_in_dim(cells, 0, width, axis=dim)
        tail = lax.slice_in_dim(cells, cells.shape[dim] - width, cells.shape[dim], axis=dim)
        cells = jnp.concatenate(
            [
                lax.ppermute(tail, axis, [(i, (i + 1) % count) for i in range(ends)]),
                cells,
                lax.ppermute(head, axis, [((i + 1) % count, i) for i in range(ends)]),
            ],
            axis=dim,
        )
    return cells


def cross_sum(field):
    padded = jnp.pad(field, ((0, 0), (0, 0), (1, 1), (1, 1)))
    beside = padded[:, :, 2:, 1:-1] + padded[:, :, :-2, 1:-1]
    beside = beside + padded[:, :, 1:-1, 2:] + padded[:, :, 1:-1, :-2]
    return beside


def gather_all(block, axis):
    count = lax.axis_size(axis)
    if count & (count - 1):
        return lax.all_gather(block, axis)
    me = lax.axis_index(axis)
    held = block[None]
    span = 1
    while span < count:
        other = lax.ppermute(held, axis, [(i, i ^ span) for i in range(count)])
        low = (me & span) == 0
        held = jnp.where(
            low,
            jnp.concatenate([held, other], axis=0),
            jnp.concatenate([other, held], axis=0),
        )
        span *= 2
    return held


def body(
    density,
    space_factor,
    diff_rate,
    loss_inverse,
    chain_yield,
    survival,
    gamma_yield,
    sky_weight,
    sky_blocks,
):
    groups = lax.axis_size("species")
    tiles = lax.axis_size("space")
    rows = NB // tiles

    yields_all = gather_all(chain_yield[0], "species")
    field = density[0]
    bins = field.shape[0]
    depth = field.shape[3]
    rate = diff_rate[0][:, None, None, None]
    factor = rate * space_factor[None]
    halo = SUBSTEPS
    count = lax.axis_size("space")
    mine = jnp.concatenate([field, space_factor[None]], axis=0)
    from_left = lax.ppermute(
        mine[:, mine.shape[1] - halo:], "space", [(i, i + 1) for i in range(count - 1)]
    )
    from_right = lax.ppermute(mine[:, :halo], "space", [(i + 1, i) for i in range(count - 1)])
    wide = jnp.concatenate([from_left[:bins], field, from_right[:bins]], axis=1)
    wide_factor = rate * jnp.concatenate([from_left[bins], space_factor, from_right[bins]], axis=0)[None]
    for step in range(SUBSTEPS):
        inner = wide[:, 1:-1]
        beside = wide[:, 2:] + wide[:, :-2] + cross_sum(inner)
        wide = inner + wide_factor[:, 1 + step:wide_factor.shape[1] - 1 - step] * (beside - 6.0 * inner)
    field = wide
    solved = jnp.dot(
        loss_inverse[0],
        field.reshape(bins, -1),
        precision=HIGH,
        preferred_element_type=jnp.float32,
    ).reshape(field.shape)
    chain = chain_yield[0]
    own_part = survival[0][:, None, None, None] * solved

    own_columns = jnp.sum(own_part, axis=3).reshape(bins, -1)
    cols = own_columns.shape[1]
    extra = jnp.zeros((2, cols), jnp.float32).at[0, :bins].set(chain).at[1, :bins].set(gamma_yield[0])
    packed = jnp.concatenate([own_columns, extra], axis=0)
    slabs = own_part.reshape((bins, own_part.shape[1], groups, -1) + own_part.shape[3:])
    slabs = jnp.moveaxis(slabs, 2, 0)
    me_s = lax.axis_index("species")
    shifts = list(range(1, groups))
    flat_packed = packed.reshape(-1)
    slab_shape = slabs.shape[1:]
    slab_size = slabs[0].size

    def message(index):
        slab = lax.dynamic_index_in_dim(slabs, index, 0, keepdims=False)
        return jnp.concatenate([slab.reshape(-1), flat_packed])

    by_shift = [message(me_s)]
    for d in shifts:
        by_shift.append(
            lax.ppermute(message((me_s + d) % groups), "species", [(i, (i + d) % groups) for i in range(groups)])
        )
    landed = jnp.take(jnp.stack(by_shift), (me_s - jnp.arange(groups)) % groups, axis=0)
    parts = landed[:, :slab_size].reshape((groups,) + slab_shape)
    everyone = landed[:, slab_size:].reshape((groups,) + packed.shape)
    sums = everyone[0, :bins]
    total = jnp.zeros((cols,), jnp.float32)
    for group in range(groups):
        if group > 0:
            sums = everyone[group, bins, :bins][:, None] * sums + everyone[group, :bins]
        weighted = jnp.dot(
            everyone[group, bins + 1, :bins], sums, precision=HIGH, preferred_element_type=jnp.float32
        )
        emission = lax.reduce_precision(weighted / (bins * depth), exponent_bits=8, mantissa_bits=7)
        total = total + emission
    contribution = jnp.einsum(
        "c,lcb->lb", total, sky_weight[0].astype(jnp.float32), precision=HIGH
    )
    lines, pixels = contribution.shape
    ids = jnp.zeros((1, pixels), jnp.float32).at[0, :lines].set(sky_blocks[0].astype(jnp.float32))
    payload = jnp.concatenate([contribution, ids], axis=0)
    running = parts[0]
    results = [running]
    for group in range(1, groups):
        running = yields_all[group][:, None, None, None] * running + parts[group]
        results.append(running)
    results = jnp.stack(results)
    back = [lax.dynamic_index_in_dim(results, me_s, 0, keepdims=False)]
    for d in shifts:
        outgoing = lax.dynamic_index_in_dim(results, (me_s + d) % groups, 0, keepdims=False)
        back.append(lax.ppermute(outgoing, "species", [(i, (i + d) % groups) for i in range(groups)]))
    mine_slabs = jnp.take(jnp.stack(back), (me_s - jnp.arange(groups)) % groups, axis=0)
    carried = jnp.moveaxis(mine_slabs, 0, 2).reshape(own_part.shape)
    gathered = gather_all(payload, "space")
    mine = lax.axis_index("space") * rows + jnp.arange(rows, dtype=jnp.int32)
    onehot = (
        gathered[:, lines, :lines].reshape(1, tiles * lines) == mine.astype(jnp.float32)[:, None]
    ).astype(jnp.float32)
    sky = jnp.dot(
        onehot,
        gathered[:, :lines].reshape(tiles * lines, pixels),
        precision=HIGH,
        preferred_element_type=jnp.float32,
    )

    return (carried[None], sky)


def solution(mesh):
    placed = (
        P("species", None, "space", None, None),
        P("space", None, None),
        P("species", None),
        P("species", None, None),
        P("species", None),
        P("species", None),
        P("species", None),
        P("space", None, None, None),
        P("space", None),
    )
    return jax.shard_map(
        body,
        mesh=mesh,
        in_specs=placed,
        out_specs=(P("species", None, "space", None, None), P("space", None)),
        check_vma=False,
    )
```

```python
import jax
import jax.numpy as jnp
from jax import lax
from jax.sharding import PartitionSpec as P

SUBSTEPS = 2
NB = 384
CHUNKS = 4
HIGH = lax.Precision.HIGHEST


def padded_2(cells, sides, width):
    for axis, dim in sides:
        count = lax.axis_size(axis)
        ends = count - 1
        head = lax.slice_in_dim(cells, 0, width, axis=dim)
        tail = lax.slice_in_dim(cells, cells.shape[dim] - width, cells.shape[dim], axis=dim)
        cells = jnp.concatenate(
            [
                lax.ppermute(tail, axis, [(i, (i + 1) % count) for i in range(ends)]),
                cells,
                lax.ppermute(head, axis, [((i + 1) % count, i) for i in range(ends)]),
            ],
            axis=dim,
        )
    return cells


def cross_sum(field):
    padded = jnp.pad(field, ((0, 0), (0, 0), (1, 1), (1, 1)))
    beside = padded[:, :, 2:, 1:-1] + padded[:, :, :-2, 1:-1]
    beside = beside + padded[:, :, 1:-1, 2:] + padded[:, :, 1:-1, :-2]
    return beside


def gather_all(block, axis):
    count = lax.axis_size(axis)
    if count & (count - 1):
        return lax.all_gather(block, axis)
    me = lax.axis_index(axis)
    held = block[None]
    span = 1
    while span < count:
        other = lax.ppermute(held, axis, [(i, i ^ span) for i in range(count)])
        low = (me & span) == 0
        held = jnp.where(
            low,
            jnp.concatenate([held, other], axis=0),
            jnp.concatenate([other, held], axis=0),
        )
        span *= 2
    return held


def body(
    density,
    space_factor,
    diff_rate,
    loss_inverse,
    chain_yield,
    survival,
    gamma_yield,
    sky_weight,
    sky_blocks,
):
    groups = lax.axis_size("species")
    tiles = lax.axis_size("space")
    rows = NB // tiles

    yields_all = gather_all(chain_yield[0], "species")
    field = density[0]
    bins = field.shape[0]
    depth = field.shape[3]
    rate = diff_rate[0][:, None, None, None]
    factor = rate * space_factor[None]
    halo = SUBSTEPS
    count = lax.axis_size("space")
    mine = jnp.concatenate([field, space_factor[None]], axis=0)
    from_left = lax.ppermute(
        mine[:, mine.shape[1] - halo:], "space", [(i, i + 1) for i in range(count - 1)]
    )
    from_right = lax.ppermute(mine[:, :halo], "space", [(i + 1, i) for i in range(count - 1)])
    wide = jnp.concatenate([from_left[:bins], field, from_right[:bins]], axis=1)
    wide_factor = rate * jnp.concatenate([from_left[bins], space_factor, from_right[bins]], axis=0)[None]
    for step in range(SUBSTEPS):
        inner = wide[:, 1:-1]
        beside = wide[:, 2:] + wide[:, :-2] + cross_sum(inner)
        wide = inner + wide_factor[:, 1 + step:wide_factor.shape[1] - 1 - step] * (beside - 6.0 * inner)
    field = wide
    solved = jnp.dot(
        loss_inverse[0],
        field.reshape(bins, -1),
        precision=HIGH,
        preferred_element_type=jnp.float32,
    ).reshape(field.shape)
    chain = chain_yield[0]
    own_part = survival[0][:, None, None, None] * solved

    own_columns = jnp.sum(own_part, axis=3).reshape(bins, -1)
    cols = own_columns.shape[1]
    extra = jnp.zeros((2, cols), jnp.float32).at[0, :bins].set(chain).at[1, :bins].set(gamma_yield[0])
    packed = jnp.concatenate([own_columns, extra], axis=0)
    slabs = own_part.reshape((bins, own_part.shape[1], groups, -1) + own_part.shape[3:])
    slabs = jnp.moveaxis(slabs, 2, 0)
    me_s = lax.axis_index("species")
    shifts = list(range(1, groups))
    flat_packed = packed.reshape(-1)
    slab_shape = slabs.shape[1:]
    slab_size = slabs[0].size

    def message(index):
        slab = lax.dynamic_index_in_dim(slabs, index, 0, keepdims=False)
        return jnp.concatenate([slab.reshape(-1), flat_packed])

    by_shift = [message(me_s)]
    for d in shifts:
        by_shift.append(
            lax.ppermute(message((me_s + d) % groups), "species", [(i, (i + d) % groups) for i in range(groups)])
        )
    landed = jnp.take(jnp.stack(by_shift), (me_s - jnp.arange(groups)) % groups, axis=0)
    parts = landed[:, :slab_size].reshape((groups,) + slab_shape)
    everyone = landed[:, slab_size:].reshape((groups,) + packed.shape)
    sums = everyone[0, :bins]
    total = jnp.zeros((cols,), jnp.float32)
    for group in range(groups):
        if group > 0:
            sums = everyone[group, bins, :bins][:, None] * sums + everyone[group, :bins]
        weighted = jnp.dot(
            everyone[group, bins + 1, :bins], sums, precision=HIGH, preferred_element_type=jnp.float32
        )
        emission = lax.reduce_precision(weighted / (bins * depth), exponent_bits=8, mantissa_bits=7)
        total = total + emission
    contribution = jnp.einsum(
        "c,lcb->lb", total, sky_weight[0].astype(jnp.float32), precision=HIGH
    )
    lines, pixels = contribution.shape
    ids = jnp.zeros((1, pixels), jnp.float32).at[0, :lines].set(sky_blocks[0].astype(jnp.float32))
    payload = jnp.concatenate([contribution, ids], axis=0)
    running = parts[0]
    results = [running]
    for group in range(1, groups):
        running = yields_all[group][:, None, None, None] * running + parts[group]
        results.append(running)
    results = jnp.stack(results)
    back = [lax.dynamic_index_in_dim(results, me_s, 0, keepdims=False)]
    for d in shifts:
        outgoing = lax.dynamic_index_in_dim(results, (me_s + d) % groups, 0, keepdims=False)
        back.append(lax.ppermute(outgoing, "species", [(i, (i + d) % groups) for i in range(groups)]))
    payload, back = lax.optimization_barrier((payload, back))
    mine_slabs = jnp.take(jnp.stack(back), (me_s - jnp.arange(groups)) % groups, axis=0)
    carried = jnp.moveaxis(mine_slabs, 0, 2).reshape(own_part.shape)
    gathered = gather_all(payload, "space")
    mine = lax.axis_index("space") * rows + jnp.arange(rows, dtype=jnp.int32)
    onehot = (
        gathered[:, lines, :lines].reshape(1, tiles * lines) == mine.astype(jnp.float32)[:, None]
    ).astype(jnp.float32)
    sky = jnp.dot(
        onehot,
        gathered[:, :lines].reshape(tiles * lines, pixels),
        precision=HIGH,
        preferred_element_type=jnp.float32,
    )

    return (carried[None], sky)


def solution(mesh):
    placed = (
        P("species", None, "space", None, None),
        P("space", None, None),
        P("species", None),
        P("species", None, None),
        P("species", None),
        P("species", None),
        P("species", None),
        P("space", None, None, None),
        P("space", None),
    )
    return jax.shard_map(
        body,
        mesh=mesh,
        in_specs=placed,
        out_specs=(P("species", None, "space", None, None), P("space", None)),
        check_vma=False,
    )
```

```python
import jax
import jax.numpy as jnp
from jax import lax
from jax.sharding import PartitionSpec as P

SUBSTEPS = 2
NB = 384
CHUNKS = 4
HIGH = lax.Precision.HIGHEST


def padded_2(cells, sides, width):
    for axis, dim in sides:
        count = lax.axis_size(axis)
        ends = count - 1
        head = lax.slice_in_dim(cells, 0, width, axis=dim)
        tail = lax.slice_in_dim(cells, cells.shape[dim] - width, cells.shape[dim], axis=dim)
        cells = jnp.concatenate(
            [
                lax.ppermute(tail, axis, [(i, (i + 1) % count) for i in range(ends)]),
                cells,
                lax.ppermute(head, axis, [((i + 1) % count, i) for i in range(ends)]),
            ],
            axis=dim,
        )
    return cells


def cross_sum(field):
    padded = jnp.pad(field, ((0, 0), (0, 0), (1, 1), (1, 1)))
    beside = padded[:, :, 2:, 1:-1] + padded[:, :, :-2, 1:-1]
    beside = beside + padded[:, :, 1:-1, 2:] + padded[:, :, 1:-1, :-2]
    return beside


def gather_all(block, axis):
    count = lax.axis_size(axis)
    if count & (count - 1):
        return lax.all_gather(block, axis)
    me = lax.axis_index(axis)
    held = block[None]
    span = 1
    while span < count:
        other = lax.ppermute(held, axis, [(i, i ^ span) for i in range(count)])
        low = (me & span) == 0
        held = jnp.where(
            low,
            jnp.concatenate([held, other], axis=0),
            jnp.concatenate([other, held], axis=0),
        )
        span *= 2
    return held


def body(
    density,
    space_factor,
    diff_rate,
    loss_inverse,
    chain_yield,
    survival,
    gamma_yield,
    sky_weight,
    sky_blocks,
):
    groups = lax.axis_size("species")
    tiles = lax.axis_size("space")
    rows = NB // tiles

    field = density[0]
    bins = field.shape[0]
    depth = field.shape[3]
    rate = diff_rate[0][:, None, None, None]
    factor = rate * space_factor[None]
    halo = SUBSTEPS
    count = lax.axis_size("space")
    mine = jnp.concatenate([field, space_factor[None]], axis=0)
    from_left = lax.ppermute(
        mine[:, mine.shape[1] - halo:], "space", [(i, i + 1) for i in range(count - 1)]
    )
    from_right = lax.ppermute(mine[:, :halo], "space", [(i + 1, i) for i in range(count - 1)])
    wide = jnp.concatenate([from_left[:bins], field, from_right[:bins]], axis=1)
    wide_factor = rate * jnp.concatenate([from_left[bins], space_factor, from_right[bins]], axis=0)[None]
    for step in range(SUBSTEPS):
        inner = wide[:, 1:-1]
        beside = wide[:, 2:] + wide[:, :-2] + cross_sum(inner)
        wide = inner + wide_factor[:, 1 + step:wide_factor.shape[1] - 1 - step] * (beside - 6.0 * inner)
    field = wide
    solved = jnp.dot(
        loss_inverse[0],
        field.reshape(bins, -1),
        precision=HIGH,
        preferred_element_type=jnp.float32,
    ).reshape(field.shape)
    chain = chain_yield[0]
    own_part = survival[0][:, None, None, None] * solved

    own_columns = jnp.sum(own_part, axis=3).reshape(bins, -1)
    cols = own_columns.shape[1]
    extra = jnp.zeros((2, cols), jnp.float32).at[0, :bins].set(chain).at[1, :bins].set(gamma_yield[0])
    packed = jnp.concatenate([own_columns, extra], axis=0)
    base = bins // CHUNKS
    bounds = [0]
    for c in range(CHUNKS):
        bounds.append(bounds[-1] + base + 2 * c - (CHUNKS - 1))
    bounds[-1] = bins
    pieces = [own_part[bounds[c]:bounds[c + 1]] for c in range(CHUNKS)]
    scales = [chain[bounds[c]:bounds[c + 1]][:, None, None, None] for c in range(CHUNKS)]
    landed = []
    for c in range(CHUNKS):
        arrived = lax.ppermute(pieces[c], "species", [(0, 1)])
        if c == 0:
            packed, arrived = lax.optimization_barrier((packed, arrived))
        landed.append(arrived)
    me_g = lax.axis_index("species")
    everyone = packed[None]
    span = 1
    while span < groups:
        other = lax.ppermute(everyone, "species", [(i, i ^ span) for i in range(groups)])
        low = (me_g & span) == 0
        everyone = jnp.where(
            low,
            jnp.concatenate([everyone, other], axis=0),
            jnp.concatenate([other, everyone], axis=0),
        )
        span *= 2
    sums = everyone[0, :bins]
    total = jnp.zeros((cols,), jnp.float32)
    for group in range(groups):
        if group > 0:
            sums = everyone[group, bins, :bins][:, None] * sums + everyone[group, :bins]
        weighted = jnp.dot(
            everyone[group, bins + 1, :bins], sums, precision=HIGH, preferred_element_type=jnp.float32
        )
        emission = lax.reduce_precision(weighted / (bins * depth), exponent_bits=8, mantissa_bits=7)
        total = total + emission
    contribution = jnp.einsum(
        "c,lcb->lb", total, sky_weight[0].astype(jnp.float32), precision=HIGH
    )
    lines, pixels = contribution.shape
    ids = jnp.zeros((1, pixels), jnp.float32).at[0, :lines].set(sky_blocks[0].astype(jnp.float32))
    payload = jnp.concatenate([contribution, ids], axis=0)
    payload, landed[-1] = lax.optimization_barrier((payload, landed[-1]))
    for c in range(CHUNKS):
        pieces[c] = pieces[c] + scales[c] * landed[c]
    for wave in range(1, CHUNKS + groups - 2):
        for c in range(CHUNKS):
            s = wave - c
            if 1 <= s < groups - 1:
                arrived = lax.ppermute(pieces[c], "species", [(s, s + 1)])
                pieces[c] = pieces[c] + scales[c] * arrived
    carried = jnp.concatenate(pieces, axis=0)
    gathered = gather_all(payload, "space")
    mine = lax.axis_index("space") * rows + jnp.arange(rows, dtype=jnp.int32)
    onehot = (
        gathered[:, lines, :lines].reshape(1, tiles * lines) == mine.astype(jnp.float32)[:, None]
    ).astype(jnp.float32)
    sky = jnp.dot(
        onehot,
        gathered[:, :lines].reshape(tiles * lines, pixels),
        precision=HIGH,
        preferred_element_type=jnp.float32,
    )

    return (carried[None], sky)


def solution(mesh):
    placed = (
        P("species", None, "space", None, None),
        P("space", None, None),
        P("species", None),
        P("species", None, None),
        P("species", None),
        P("species", None),
        P("species", None),
        P("space", None, None, None),
        P("space", None),
    )
    return jax.shard_map(
        body,
        mesh=mesh,
        in_specs=placed,
        out_specs=(P("species", None, "space", None, None), P("space", None)),
        check_vma=False,
    )
```

```python
import jax
import jax.numpy as jnp
from jax import lax
from jax.sharding import PartitionSpec as P

SUBSTEPS = 2
NB = 384
CHUNKS = 4
HIGH = lax.Precision.HIGHEST


def padded_2(cells, sides, width):
    for axis, dim in sides:
        count = lax.axis_size(axis)
        ends = count - 1
        head = lax.slice_in_dim(cells, 0, width, axis=dim)
        tail = lax.slice_in_dim(cells, cells.shape[dim] - width, cells.shape[dim], axis=dim)
        cells = jnp.concatenate(
            [
                lax.ppermute(tail, axis, [(i, (i + 1) % count) for i in range(ends)]),
                cells,
                lax.ppermute(head, axis, [((i + 1) % count, i) for i in range(ends)]),
            ],
            axis=dim,
        )
    return cells


def cross_sum(field):
    padded = jnp.pad(field, ((0, 0), (0, 0), (1, 1), (1, 1)))
    beside = padded[:, :, 2:, 1:-1] + padded[:, :, :-2, 1:-1]
    beside = beside + padded[:, :, 1:-1, 2:] + padded[:, :, 1:-1, :-2]
    return beside


def gather_all(block, axis):
    count = lax.axis_size(axis)
    if count & (count - 1):
        return lax.all_gather(block, axis)
    me = lax.axis_index(axis)
    held = block[None]
    span = 1
    while span < count:
        other = lax.ppermute(held, axis, [(i, i ^ span) for i in range(count)])
        low = (me & span) == 0
        held = jnp.where(
            low,
            jnp.concatenate([held, other], axis=0),
            jnp.concatenate([other, held], axis=0),
        )
        span *= 2
    return held


def body(
    density,
    space_factor,
    diff_rate,
    loss_inverse,
    chain_yield,
    survival,
    gamma_yield,
    sky_weight,
    sky_blocks,
):
    groups = lax.axis_size("species")
    tiles = lax.axis_size("space")
    rows = NB // tiles

    yields_all = gather_all(chain_yield[0], "species")
    field = density[0]
    bins = field.shape[0]
    depth = field.shape[3]
    rate = diff_rate[0][:, None, None, None]
    factor = rate * space_factor[None]
    halo = SUBSTEPS
    count = lax.axis_size("space")
    mine = jnp.concatenate([field, space_factor[None]], axis=0)
    from_left = lax.ppermute(
        mine[:, mine.shape[1] - halo:], "space", [(i, i + 1) for i in range(count - 1)]
    )
    from_right = lax.ppermute(mine[:, :halo], "space", [(i + 1, i) for i in range(count - 1)])
    wide = jnp.concatenate([from_left[:bins], field, from_right[:bins]], axis=1)
    wide_factor = rate * jnp.concatenate([from_left[bins], space_factor, from_right[bins]], axis=0)[None]
    for step in range(SUBSTEPS):
        inner = wide[:, 1:-1]
        beside = wide[:, 2:] + wide[:, :-2] + cross_sum(inner)
        wide = inner + wide_factor[:, 1 + step:wide_factor.shape[1] - 1 - step] * (beside - 6.0 * inner)
    field = wide
    solved = jnp.dot(
        loss_inverse[0],
        field.reshape(bins, -1),
        precision=HIGH,
        preferred_element_type=jnp.float32,
    ).reshape(field.shape)
    chain = chain_yield[0]
    own_part = survival[0][:, None, None, None] * solved

    own_columns = jnp.sum(own_part, axis=3).reshape(bins, -1)
    cols = own_columns.shape[1]
    extra = jnp.zeros((2, cols), jnp.float32).at[0, :bins].set(chain).at[1, :bins].set(gamma_yield[0])
    packed = jnp.concatenate([own_columns, extra], axis=0)
    slabs = own_part.reshape((bins, own_part.shape[1], groups, -1) + own_part.shape[3:])
    slabs = jnp.moveaxis(slabs, 2, 0)
    me_s = lax.axis_index("species")
    shifts = list(range(1, groups))
    flat_packed = packed.reshape(-1)
    slab_shape = slabs.shape[1:]
    slab_size = slabs[0].size

    def message(index):
        slab = lax.dynamic_index_in_dim(slabs, index, 0, keepdims=False)
        return jnp.concatenate([slab.reshape(-1), flat_packed])

    by_shift = [message(me_s)]
    for d in shifts:
        by_shift.append(
            lax.ppermute(message((me_s + d) % groups), "species", [(i, (i + d) % groups) for i in range(groups)])
        )
    landed = jnp.take(jnp.stack(by_shift), (me_s - jnp.arange(groups)) % groups, axis=0)
    parts = landed[:, :slab_size].reshape((groups,) + slab_shape)
    everyone = landed[:, slab_size:].reshape((groups,) + packed.shape)
    sums = everyone[0, :bins]
    total = jnp.zeros((cols,), jnp.float32)
    for group in range(groups):
        if group > 0:
            sums = everyone[group, bins, :bins][:, None] * sums + everyone[group, :bins]
        weighted = jnp.dot(
            everyone[group, bins + 1, :bins], sums, precision=HIGH, preferred_element_type=jnp.float32
        )
        emission = lax.reduce_precision(weighted / (bins * depth), exponent_bits=8, mantissa_bits=7)
        total = total + emission
    contribution = jnp.einsum(
        "c,lcb->lb", total, sky_weight[0].astype(jnp.float32), precision=HIGH
    )
    lines, pixels = contribution.shape
    ids = jnp.zeros((1, pixels), jnp.float32).at[0, :lines].set(sky_blocks[0].astype(jnp.float32))
    payload = jnp.concatenate([contribution, ids], axis=0)
    running = parts[0]
    results = [running]
    for group in range(1, groups):
        running = yields_all[group][:, None, None, None] * running + parts[group]
        results.append(running)
    results = jnp.stack(results)
    back = [lax.dynamic_index_in_dim(results, me_s, 0, keepdims=False)]
    for d in shifts:
        outgoing = lax.dynamic_index_in_dim(results, (me_s + d) % groups, 0, keepdims=False)
        back.append(lax.ppermute(outgoing, "species", [(i, (i + d) % groups) for i in range(groups)]))
    payload, back[1] = lax.optimization_barrier((payload, back[1]))
    mine_slabs = jnp.take(jnp.stack(back), (me_s - jnp.arange(groups)) % groups, axis=0)
    carried = jnp.moveaxis(mine_slabs, 0, 2).reshape(own_part.shape)
    gathered = gather_all(payload, "space")
    mine = lax.axis_index("space") * rows + jnp.arange(rows, dtype=jnp.int32)
    onehot = (
        gathered[:, lines, :lines].reshape(1, tiles * lines) == mine.astype(jnp.float32)[:, None]
    ).astype(jnp.float32)
    sky = jnp.dot(
        onehot,
        gathered[:, :lines].reshape(tiles * lines, pixels),
        precision=HIGH,
        preferred_element_type=jnp.float32,
    )

    return (carried[None], sky)


def solution(mesh):
    placed = (
        P("species", None, "space", None, None),
        P("space", None, None),
        P("species", None),
        P("species", None, None),
        P("species", None),
        P("species", None),
        P("species", None),
        P("space", None, None, None),
        P("space", None),
    )
    return jax.shard_map(
        body,
        mesh=mesh,
        in_specs=placed,
        out_specs=(P("species", None, "space", None, None), P("space", None)),
        check_vma=False,
    )
```

```python
import jax
import jax.numpy as jnp
from jax import lax
from jax.sharding import PartitionSpec as P

SUBSTEPS = 2
NB = 384
CHUNKS = 4
HIGH = lax.Precision.HIGHEST


def padded_2(cells, sides, width):
    for axis, dim in sides:
        count = lax.axis_size(axis)
        ends = count - 1
        head = lax.slice_in_dim(cells, 0, width, axis=dim)
        tail = lax.slice_in_dim(cells, cells.shape[dim] - width, cells.shape[dim], axis=dim)
        cells = jnp.concatenate(
            [
                lax.ppermute(tail, axis, [(i, (i + 1) % count) for i in range(ends)]),
                cells,
                lax.ppermute(head, axis, [((i + 1) % count, i) for i in range(ends)]),
            ],
            axis=dim,
        )
    return cells


def cross_sum(field):
    padded = jnp.pad(field, ((0, 0), (0, 0), (1, 1), (1, 1)))
    beside = padded[:, :, 2:, 1:-1] + padded[:, :, :-2, 1:-1]
    beside = beside + padded[:, :, 1:-1, 2:] + padded[:, :, 1:-1, :-2]
    return beside


def gather_all(block, axis):
    count = lax.axis_size(axis)
    if count & (count - 1):
        return lax.all_gather(block, axis)
    me = lax.axis_index(axis)
    held = block[None]
    span = 1
    while span < count:
        other = lax.ppermute(held, axis, [(i, i ^ span) for i in range(count)])
        low = (me & span) == 0
        held = jnp.where(
            low,
            jnp.concatenate([held, other], axis=0),
            jnp.concatenate([other, held], axis=0),
        )
        span *= 2
    return held


def body(
    density,
    space_factor,
    diff_rate,
    loss_inverse,
    chain_yield,
    survival,
    gamma_yield,
    sky_weight,
    sky_blocks,
):
    groups = lax.axis_size("species")
    tiles = lax.axis_size("space")
    rows = NB // tiles

    yields_all = gather_all(chain_yield[0], "species")
    field = density[0]
    bins = field.shape[0]
    depth = field.shape[3]
    rate = diff_rate[0][:, None, None, None]
    factor = rate * space_factor[None]
    halo = SUBSTEPS
    count = lax.axis_size("space")
    mine = jnp.concatenate([field, space_factor[None]], axis=0)
    from_left = lax.ppermute(
        mine[:, mine.shape[1] - halo:], "space", [(i, i + 1) for i in range(count - 1)]
    )
    from_right = lax.ppermute(mine[:, :halo], "space", [(i + 1, i) for i in range(count - 1)])
    wide = jnp.concatenate([from_left[:bins], field, from_right[:bins]], axis=1)
    wide_factor = rate * jnp.concatenate([from_left[bins], space_factor, from_right[bins]], axis=0)[None]
    for step in range(SUBSTEPS):
        inner = wide[:, 1:-1]
        beside = wide[:, 2:] + wide[:, :-2] + cross_sum(inner)
        wide = inner + wide_factor[:, 1 + step:wide_factor.shape[1] - 1 - step] * (beside - 6.0 * inner)
    field = wide
    solved = jnp.dot(
        loss_inverse[0],
        field.reshape(bins, -1),
        precision=HIGH,
        preferred_element_type=jnp.float32,
    ).reshape(field.shape)
    chain = chain_yield[0]
    own_part = survival[0][:, None, None, None] * solved

    own_columns = jnp.sum(own_part, axis=3).reshape(bins, -1)
    cols = own_columns.shape[1]
    extra = jnp.zeros((2, cols), jnp.float32).at[0, :bins].set(chain).at[1, :bins].set(gamma_yield[0])
    packed = jnp.concatenate([own_columns, extra], axis=0)
    slabs = own_part.reshape((bins, own_part.shape[1], groups, -1) + own_part.shape[3:])
    slabs = jnp.moveaxis(slabs, 2, 0)
    me_s = lax.axis_index("species")
    shifts = list(range(1, groups))
    flat_packed = packed.reshape(-1)
    slab_shape = slabs.shape[1:]
    slab_size = slabs[0].size

    def message(index):
        slab = lax.dynamic_index_in_dim(slabs, index, 0, keepdims=False)
        return jnp.concatenate([slab.reshape(-1), flat_packed])

    by_shift = [message(me_s)]
    for d in shifts:
        by_shift.append(
            lax.ppermute(message((me_s + d) % groups), "species", [(i, (i + d) % groups) for i in range(groups)])
        )
    landed = jnp.take(jnp.stack(by_shift), (me_s - jnp.arange(groups)) % groups, axis=0)
    parts = landed[:, :slab_size].reshape((groups,) + slab_shape)
    everyone = landed[:, slab_size:].reshape((groups,) + packed.shape)
    sums = everyone[0, :bins]
    total = jnp.zeros((cols,), jnp.float32)
    for group in range(groups):
        if group > 0:
            sums = everyone[group, bins, :bins][:, None] * sums + everyone[group, :bins]
        weighted = jnp.dot(
            everyone[group, bins + 1, :bins], sums, precision=HIGH, preferred_element_type=jnp.float32
        )
        emission = lax.reduce_precision(weighted / (bins * depth), exponent_bits=8, mantissa_bits=7)
        total = total + emission
    contribution = jnp.einsum(
        "c,lcb->lb", total, sky_weight[0].astype(jnp.float32), precision=HIGH
    )
    lines, pixels = contribution.shape
    ids = jnp.zeros((1, pixels), jnp.float32).at[0, :lines].set(sky_blocks[0].astype(jnp.float32))
    payload = jnp.concatenate([contribution, ids], axis=0)
    running = parts[0]
    results = [running]
    for group in range(1, groups):
        running = yields_all[group][:, None, None, None] * running + parts[group]
        results.append(running)
    results = jnp.stack(results)
    back = [lax.dynamic_index_in_dim(results, me_s, 0, keepdims=False)]
    for d in shifts:
        outgoing = lax.dynamic_index_in_dim(results, (me_s + d) % groups, 0, keepdims=False)
        back.append(lax.ppermute(outgoing, "species", [(i, (i + d) % groups) for i in range(groups)]))
    payload, back[-1] = lax.optimization_barrier((payload, back[-1]))
    mine_slabs = jnp.take(jnp.stack(back), (me_s - jnp.arange(groups)) % groups, axis=0)
    carried = jnp.moveaxis(mine_slabs, 0, 2).reshape(own_part.shape)
    gathered = gather_all(payload, "space")
    mine = lax.axis_index("space") * rows + jnp.arange(rows, dtype=jnp.int32)
    onehot = (
        gathered[:, lines, :lines].reshape(1, tiles * lines) == mine.astype(jnp.float32)[:, None]
    ).astype(jnp.float32)
    sky = jnp.dot(
        onehot,
        gathered[:, :lines].reshape(tiles * lines, pixels),
        precision=HIGH,
        preferred_element_type=jnp.float32,
    )

    return (carried[None], sky)


def solution(mesh):
    placed = (
        P("species", None, "space", None, None),
        P("space", None, None),
        P("species", None),
        P("species", None, None),
        P("species", None),
        P("species", None),
        P("species", None),
        P("space", None, None, None),
        P("space", None),
    )
    return jax.shard_map(
        body,
        mesh=mesh,
        in_specs=placed,
        out_specs=(P("species", None, "space", None, None), P("space", None)),
        check_vma=False,
    )
```

```python
import jax
import jax.numpy as jnp
from jax import lax
from jax.sharding import PartitionSpec as P

SUBSTEPS = 2
NB = 384
CHUNKS = 4
HIGH = lax.Precision.HIGHEST


def padded_2(cells, sides, width):
    for axis, dim in sides:
        count = lax.axis_size(axis)
        ends = count - 1
        head = lax.slice_in_dim(cells, 0, width, axis=dim)
        tail = lax.slice_in_dim(cells, cells.shape[dim] - width, cells.shape[dim], axis=dim)
        cells = jnp.concatenate(
            [
                lax.ppermute(tail, axis, [(i, (i + 1) % count) for i in range(ends)]),
                cells,
                lax.ppermute(head, axis, [((i + 1) % count, i) for i in range(ends)]),
            ],
            axis=dim,
        )
    return cells


def cross_sum(field):
    padded = jnp.pad(field, ((0, 0), (0, 0), (1, 1), (1, 1)))
    beside = padded[:, :, 2:, 1:-1] + padded[:, :, :-2, 1:-1]
    beside = beside + padded[:, :, 1:-1, 2:] + padded[:, :, 1:-1, :-2]
    return beside


def gather_all(block, axis):
    count = lax.axis_size(axis)
    if count & (count - 1):
        return lax.all_gather(block, axis)
    me = lax.axis_index(axis)
    held = block[None]
    span = 1
    while span < count:
        other = lax.ppermute(held, axis, [(i, i ^ span) for i in range(count)])
        low = (me & span) == 0
        held = jnp.where(
            low,
            jnp.concatenate([held, other], axis=0),
            jnp.concatenate([other, held], axis=0),
        )
        span *= 2
    return held


def body(
    density,
    space_factor,
    diff_rate,
    loss_inverse,
    chain_yield,
    survival,
    gamma_yield,
    sky_weight,
    sky_blocks,
):
    groups = lax.axis_size("species")
    tiles = lax.axis_size("space")
    rows = NB // tiles

    field = density[0]
    bins = field.shape[0]
    depth = field.shape[3]
    rate = diff_rate[0][:, None, None, None]
    factor = rate * space_factor[None]
    halo = SUBSTEPS
    count = lax.axis_size("space")
    right_pairs = [(i, i + 1) for i in range(count - 1)]
    left_pairs = [(i + 1, i) for i in range(count - 1)]
    layers = field.shape[1]
    from_left = lax.ppermute(field[:, layers - halo:], "space", right_pairs)
    from_right = lax.ppermute(field[:, :halo], "space", left_pairs)
    factor_left = lax.ppermute(space_factor[layers - halo:], "space", right_pairs)
    factor_right = lax.ppermute(space_factor[:halo], "space", left_pairs)
    wide = jnp.concatenate([from_left, field, from_right], axis=1)
    wide_factor = rate * jnp.concatenate([factor_left, space_factor, factor_right], axis=0)[None]
    for step in range(SUBSTEPS):
        inner = wide[:, 1:-1]
        beside = wide[:, 2:] + wide[:, :-2] + cross_sum(inner)
        wide = inner + wide_factor[:, 1 + step:wide_factor.shape[1] - 1 - step] * (beside - 6.0 * inner)
    field = wide
    solved = jnp.dot(
        loss_inverse[0],
        field.reshape(bins, -1),
        precision=HIGH,
        preferred_element_type=jnp.float32,
    ).reshape(field.shape)
    chain = chain_yield[0]
    own_part = survival[0][:, None, None, None] * solved

    own_columns = jnp.sum(own_part, axis=3).reshape(bins, -1)
    cols = own_columns.shape[1]
    extra = jnp.zeros((2, cols), jnp.float32).at[0, :bins].set(chain).at[1, :bins].set(gamma_yield[0])
    packed = jnp.concatenate([own_columns, extra], axis=0)
    me_g = lax.axis_index("species")
    everyone = packed[None]
    span = 1
    while span < groups:
        other = lax.ppermute(everyone, "species", [(i, i ^ span) for i in range(groups)])
        if span == 1:
            own_part, other = lax.optimization_barrier((own_part, other))
        low = (me_g & span) == 0
        everyone = jnp.where(
            low,
            jnp.concatenate([everyone, other], axis=0),
            jnp.concatenate([other, everyone], axis=0),
        )
        span *= 2
    sums = everyone[0, :bins]
    total = jnp.zeros((cols,), jnp.float32)
    for group in range(groups):
        if group > 0:
            sums = everyone[group, bins, :bins][:, None] * sums + everyone[group, :bins]
        weighted = jnp.dot(
            everyone[group, bins + 1, :bins], sums, precision=HIGH, preferred_element_type=jnp.float32
        )
        emission = lax.reduce_precision(weighted / (bins * depth), exponent_bits=8, mantissa_bits=7)
        total = total + emission
    contribution = jnp.einsum(
        "c,lcb->lb", total, sky_weight[0].astype(jnp.float32), precision=HIGH
    )
    lines, pixels = contribution.shape
    ids = jnp.zeros((1, pixels), jnp.float32).at[0, :lines].set(sky_blocks[0].astype(jnp.float32))
    payload = jnp.concatenate([contribution, ids], axis=0)
    base = bins // CHUNKS
    bounds = [0]
    for c in range(CHUNKS):
        bounds.append(bounds[-1] + base + 2 * c - (CHUNKS - 1))
    bounds[-1] = bins
    pieces = [own_part[bounds[c]:bounds[c + 1]] for c in range(CHUNKS)]
    scales = [chain[bounds[c]:bounds[c + 1]][:, None, None, None] for c in range(CHUNKS)]
    for wave in range(CHUNKS + groups - 2):
        for c in range(CHUNKS):
            s = wave - c
            if 0 <= s < groups - 1:
                arrived = lax.ppermute(pieces[c], "species", [(s, s + 1)])
                if s == 0 and c == CHUNKS - 1:
                    payload, arrived = lax.optimization_barrier((payload, arrived))
                pieces[c] = pieces[c] + scales[c] * arrived
    carried = jnp.concatenate(pieces, axis=0)
    gathered = gather_all(payload, "space")
    mine = lax.axis_index("space") * rows + jnp.arange(rows, dtype=jnp.int32)
    onehot = (
        gathered[:, lines, :lines].reshape(1, tiles * lines) == mine.astype(jnp.float32)[:, None]
    ).astype(jnp.float32)
    sky = jnp.dot(
        onehot,
        gathered[:, :lines].reshape(tiles * lines, pixels),
        precision=HIGH,
        preferred_element_type=jnp.float32,
    )

    return (carried[None], sky)


def solution(mesh):
    placed = (
        P("species", None, "space", None, None),
        P("space", None, None),
        P("species", None),
        P("species", None, None),
        P("species", None),
        P("species", None),
        P("species", None),
        P("space", None, None, None),
        P("space", None),
    )
    return jax.shard_map(
        body,
        mesh=mesh,
        in_specs=placed,
        out_specs=(P("species", None, "space", None, None), P("space", None)),
        check_vma=False,
    )
```

```python
import jax
import jax.numpy as jnp
from jax import lax
from jax.sharding import PartitionSpec as P

SUBSTEPS = 2
NB = 384
CHUNKS = 4
HIGH = lax.Precision.HIGHEST


def padded_2(cells, sides, width):
    for axis, dim in sides:
        count = lax.axis_size(axis)
        ends = count - 1
        head = lax.slice_in_dim(cells, 0, width, axis=dim)
        tail = lax.slice_in_dim(cells, cells.shape[dim] - width, cells.shape[dim], axis=dim)
        cells = jnp.concatenate(
            [
                lax.ppermute(tail, axis, [(i, (i + 1) % count) for i in range(ends)]),
                cells,
                lax.ppermute(head, axis, [((i + 1) % count, i) for i in range(ends)]),
            ],
            axis=dim,
        )
    return cells


def cross_sum(field):
    padded = jnp.pad(field, ((0, 0), (0, 0), (1, 1), (1, 1)))
    beside = padded[:, :, 2:, 1:-1] + padded[:, :, :-2, 1:-1]
    beside = beside + padded[:, :, 1:-1, 2:] + padded[:, :, 1:-1, :-2]
    return beside


def gather_all(block, axis):
    count = lax.axis_size(axis)
    if count & (count - 1):
        return lax.all_gather(block, axis)
    me = lax.axis_index(axis)
    held = block[None]
    span = 1
    while span < count:
        other = lax.ppermute(held, axis, [(i, i ^ span) for i in range(count)])
        low = (me & span) == 0
        held = jnp.where(
            low,
            jnp.concatenate([held, other], axis=0),
            jnp.concatenate([other, held], axis=0),
        )
        span *= 2
    return held


def body(
    density,
    space_factor,
    diff_rate,
    loss_inverse,
    chain_yield,
    survival,
    gamma_yield,
    sky_weight,
    sky_blocks,
):
    groups = lax.axis_size("species")
    tiles = lax.axis_size("space")
    rows = NB // tiles

    field = density[0]
    bins = field.shape[0]
    depth = field.shape[3]
    rate = diff_rate[0][:, None, None, None]
    factor = rate * space_factor[None]
    halo = SUBSTEPS
    count = lax.axis_size("space")
    right_pairs = [(i, i + 1) for i in range(count - 1)]
    left_pairs = [(i + 1, i) for i in range(count - 1)]
    layers = field.shape[1]
    from_left = lax.ppermute(field[:, layers - halo:], "space", right_pairs)
    from_right = lax.ppermute(field[:, :halo], "space", left_pairs)
    factor_left = lax.ppermute(space_factor[layers - halo:], "space", right_pairs)
    factor_right = lax.ppermute(space_factor[:halo], "space", left_pairs)
    wide = jnp.concatenate([from_left, field, from_right], axis=1)
    wide_factor = rate * jnp.concatenate([factor_left, space_factor, factor_right], axis=0)[None]
    for step in range(SUBSTEPS):
        inner = wide[:, 1:-1]
        beside = wide[:, 2:] + wide[:, :-2] + cross_sum(inner)
        wide = inner + wide_factor[:, 1 + step:wide_factor.shape[1] - 1 - step] * (beside - 6.0 * inner)
    field = wide
    solved = jnp.dot(
        loss_inverse[0],
        field.reshape(bins, -1),
        precision=HIGH,
        preferred_element_type=jnp.float32,
    ).reshape(field.shape)
    chain = chain_yield[0]
    own_part = survival[0][:, None, None, None] * solved

    own_columns = jnp.sum(own_part, axis=3).reshape(bins, -1)
    cols = own_columns.shape[1]
    extra = jnp.zeros((2, cols), jnp.float32).at[0, :bins].set(chain).at[1, :bins].set(gamma_yield[0])
    packed = jnp.concatenate([own_columns, extra], axis=0)
    me_g = lax.axis_index("species")
    everyone = packed[None]
    span = 1
    while span < groups:
        other = lax.ppermute(everyone, "species", [(i, i ^ span) for i in range(groups)])
        if span == 1:
            own_part, other = lax.optimization_barrier((own_part, other))
        low = (me_g & span) == 0
        everyone = jnp.where(
            low,
            jnp.concatenate([everyone, other], axis=0),
            jnp.concatenate([other, everyone], axis=0),
        )
        span *= 2
    sums = everyone[0, :bins]
    total = jnp.zeros((cols,), jnp.float32)
    for group in range(groups):
        if group > 0:
            sums = everyone[group, bins, :bins][:, None] * sums + everyone[group, :bins]
        weighted = jnp.dot(
            everyone[group, bins + 1, :bins], sums, precision=HIGH, preferred_element_type=jnp.float32
        )
        emission = lax.reduce_precision(weighted / (bins * depth), exponent_bits=8, mantissa_bits=7)
        total = total + emission
    contribution = jnp.einsum(
        "c,lcb->lb", total, sky_weight[0].astype(jnp.float32), precision=HIGH
    )
    lines, pixels = contribution.shape
    ids = jnp.zeros((1, pixels), jnp.float32).at[0, :lines].set(sky_blocks[0].astype(jnp.float32))
    payload = jnp.concatenate([contribution, ids], axis=0)
    base = bins // CHUNKS
    bounds = [0]
    for c in range(CHUNKS):
        bounds.append(bounds[-1] + base + 2 * c - (CHUNKS - 1))
    bounds[-1] = bins
    pieces = [own_part[bounds[c]:bounds[c + 1]] for c in range(CHUNKS)]
    scales = [chain[bounds[c]:bounds[c + 1]][:, None, None, None] for c in range(CHUNKS)]
    for wave in range(CHUNKS + groups - 2):
        for c in range(CHUNKS):
            s = wave - c
            if 0 <= s < groups - 1:
                arrived = lax.ppermute(pieces[c], "species", [(s, s + 1)])
                if s == 0 and c == CHUNKS - 1:
                    payload, arrived = lax.optimization_barrier((payload, arrived))
                pieces[c] = pieces[c] + scales[c] * arrived
    carried = own_part
    for c in range(CHUNKS):
        carried = lax.dynamic_update_slice_in_dim(carried, pieces[c], bounds[c], axis=0)
    gathered = gather_all(payload, "space")
    mine = lax.axis_index("space") * rows + jnp.arange(rows, dtype=jnp.int32)
    onehot = (
        gathered[:, lines, :lines].reshape(1, tiles * lines) == mine.astype(jnp.float32)[:, None]
    ).astype(jnp.float32)
    sky = jnp.dot(
        onehot,
        gathered[:, :lines].reshape(tiles * lines, pixels),
        precision=HIGH,
        preferred_element_type=jnp.float32,
    )

    return (carried[None], sky)


def solution(mesh):
    placed = (
        P("species", None, "space", None, None),
        P("space", None, None),
        P("species", None),
        P("species", None, None),
        P("species", None),
        P("species", None),
        P("species", None),
        P("space", None, None, None),
        P("space", None),
    )
    return jax.shard_map(
        body,
        mesh=mesh,
        in_specs=placed,
        out_specs=(P("species", None, "space", None, None), P("space", None)),
        check_vma=False,
    )
```

```python
import jax
import jax.numpy as jnp
from jax import lax
from jax.sharding import PartitionSpec as P

SUBSTEPS = 2
NB = 384
CHUNKS = 4
HIGH = lax.Precision.HIGHEST


def padded_2(cells, sides, width):
    for axis, dim in sides:
        count = lax.axis_size(axis)
        ends = count - 1
        head = lax.slice_in_dim(cells, 0, width, axis=dim)
        tail = lax.slice_in_dim(cells, cells.shape[dim] - width, cells.shape[dim], axis=dim)
        cells = jnp.concatenate(
            [
                lax.ppermute(tail, axis, [(i, (i + 1) % count) for i in range(ends)]),
                cells,
                lax.ppermute(head, axis, [((i + 1) % count, i) for i in range(ends)]),
            ],
            axis=dim,
        )
    return cells


def cross_sum(field):
    padded = jnp.pad(field, ((0, 0), (0, 0), (1, 1), (1, 1)))
    beside = padded[:, :, 2:, 1:-1] + padded[:, :, :-2, 1:-1]
    beside = beside + padded[:, :, 1:-1, 2:] + padded[:, :, 1:-1, :-2]
    return beside


def gather_all(block, axis):
    count = lax.axis_size(axis)
    if count & (count - 1):
        return lax.all_gather(block, axis)
    me = lax.axis_index(axis)
    held = block[None]
    span = 1
    while span < count:
        other = lax.ppermute(held, axis, [(i, i ^ span) for i in range(count)])
        low = (me & span) == 0
        held = jnp.where(
            low,
            jnp.concatenate([held, other], axis=0),
            jnp.concatenate([other, held], axis=0),
        )
        span *= 2
    return held


def body(
    density,
    space_factor,
    diff_rate,
    loss_inverse,
    chain_yield,
    survival,
    gamma_yield,
    sky_weight,
    sky_blocks,
):
    groups = lax.axis_size("species")
    tiles = lax.axis_size("space")
    rows = NB // tiles

    field = density[0]
    bins = field.shape[0]
    depth = field.shape[3]
    rate = diff_rate[0][:, None, None, None]
    factor = rate * space_factor[None]
    halo = SUBSTEPS
    count = lax.axis_size("space")
    right_pairs = [(i, i + 1) for i in range(count - 1)]
    left_pairs = [(i + 1, i) for i in range(count - 1)]
    layers = field.shape[1]
    from_left = lax.ppermute(field[:, layers - halo:], "space", right_pairs)
    from_right = lax.ppermute(field[:, :halo], "space", left_pairs)
    factor_left = lax.ppermute(space_factor[layers - halo:], "space", right_pairs)
    factor_right = lax.ppermute(space_factor[:halo], "space", left_pairs)
    wide = jnp.concatenate([from_left, field, from_right], axis=1)
    wide_factor = rate * jnp.concatenate([factor_left, space_factor, factor_right], axis=0)[None]
    for step in range(SUBSTEPS):
        inner = wide[:, 1:-1]
        beside = wide[:, 2:] + wide[:, :-2] + cross_sum(inner)
        wide = inner + wide_factor[:, 1 + step:wide_factor.shape[1] - 1 - step] * (beside - 6.0 * inner)
    field = wide
    solved = jnp.dot(
        loss_inverse[0],
        field.reshape(bins, -1),
        precision=lax.Precision.HIGH,
        preferred_element_type=jnp.float32,
    ).reshape(field.shape)
    chain = chain_yield[0]
    own_part = survival[0][:, None, None, None] * solved

    own_columns = jnp.sum(own_part, axis=3).reshape(bins, -1)
    cols = own_columns.shape[1]
    extra = jnp.zeros((2, cols), jnp.float32).at[0, :bins].set(chain).at[1, :bins].set(gamma_yield[0])
    packed = jnp.concatenate([own_columns, extra], axis=0)
    me_g = lax.axis_index("species")
    everyone = packed[None]
    span = 1
    while span < groups:
        other = lax.ppermute(everyone, "species", [(i, i ^ span) for i in range(groups)])
        if span == 1:
            own_part, other = lax.optimization_barrier((own_part, other))
        low = (me_g & span) == 0
        everyone = jnp.where(
            low,
            jnp.concatenate([everyone, other], axis=0),
            jnp.concatenate([other, everyone], axis=0),
        )
        span *= 2
    sums = everyone[0, :bins]
    total = jnp.zeros((cols,), jnp.float32)
    for group in range(groups):
        if group > 0:
            sums = everyone[group, bins, :bins][:, None] * sums + everyone[group, :bins]
        weighted = jnp.dot(
            everyone[group, bins + 1, :bins], sums, precision=HIGH, preferred_element_type=jnp.float32
        )
        emission = lax.reduce_precision(weighted / (bins * depth), exponent_bits=8, mantissa_bits=7)
        total = total + emission
    contribution = jnp.einsum(
        "c,lcb->lb", total, sky_weight[0].astype(jnp.float32), precision=HIGH
    )
    lines, pixels = contribution.shape
    ids = jnp.zeros((1, pixels), jnp.float32).at[0, :lines].set(sky_blocks[0].astype(jnp.float32))
    payload = jnp.concatenate([contribution, ids], axis=0)
    base = bins // CHUNKS
    bounds = [0]
    for c in range(CHUNKS):
        bounds.append(bounds[-1] + base + 2 * c - (CHUNKS - 1))
    bounds[-1] = bins
    pieces = [own_part[bounds[c]:bounds[c + 1]] for c in range(CHUNKS)]
    scales = [chain[bounds[c]:bounds[c + 1]][:, None, None, None] for c in range(CHUNKS)]
    for wave in range(CHUNKS + groups - 2):
        for c in range(CHUNKS):
            s = wave - c
            if 0 <= s < groups - 1:
                arrived = lax.ppermute(pieces[c], "species", [(s, s + 1)])
                if s == 0 and c == CHUNKS - 1:
                    payload, arrived = lax.optimization_barrier((payload, arrived))
                pieces[c] = pieces[c] + scales[c] * arrived
    carried = jnp.concatenate(pieces, axis=0)
    gathered = gather_all(payload, "space")
    mine = lax.axis_index("space") * rows + jnp.arange(rows, dtype=jnp.int32)
    onehot = (
        gathered[:, lines, :lines].reshape(1, tiles * lines) == mine.astype(jnp.float32)[:, None]
    ).astype(jnp.float32)
    sky = jnp.dot(
        onehot,
        gathered[:, :lines].reshape(tiles * lines, pixels),
        precision=HIGH,
        preferred_element_type=jnp.float32,
    )

    return (carried[None], sky)


def solution(mesh):
    placed = (
        P("species", None, "space", None, None),
        P("space", None, None),
        P("species", None),
        P("species", None, None),
        P("species", None),
        P("species", None),
        P("species", None),
        P("space", None, None, None),
        P("space", None),
    )
    return jax.shard_map(
        body,
        mesh=mesh,
        in_specs=placed,
        out_specs=(P("species", None, "space", None, None), P("space", None)),
        check_vma=False,
    )
```

```python
import jax
import jax.numpy as jnp
from jax import lax
from jax.sharding import PartitionSpec as P

SUBSTEPS = 2
NB = 384
CHUNKS = 4
HIGH = lax.Precision.HIGH


def padded_2(cells, sides, width):
    for axis, dim in sides:
        count = lax.axis_size(axis)
        ends = count - 1
        head = lax.slice_in_dim(cells, 0, width, axis=dim)
        tail = lax.slice_in_dim(cells, cells.shape[dim] - width, cells.shape[dim], axis=dim)
        cells = jnp.concatenate(
            [
                lax.ppermute(tail, axis, [(i, (i + 1) % count) for i in range(ends)]),
                cells,
                lax.ppermute(head, axis, [((i + 1) % count, i) for i in range(ends)]),
            ],
            axis=dim,
        )
    return cells


def cross_sum(field):
    padded = jnp.pad(field, ((0, 0), (0, 0), (1, 1), (1, 1)))
    beside = padded[:, :, 2:, 1:-1] + padded[:, :, :-2, 1:-1]
    beside = beside + padded[:, :, 1:-1, 2:] + padded[:, :, 1:-1, :-2]
    return beside


def gather_all(block, axis):
    count = lax.axis_size(axis)
    if count & (count - 1):
        return lax.all_gather(block, axis)
    me = lax.axis_index(axis)
    held = block[None]
    span = 1
    while span < count:
        other = lax.ppermute(held, axis, [(i, i ^ span) for i in range(count)])
        low = (me & span) == 0
        held = jnp.where(
            low,
            jnp.concatenate([held, other], axis=0),
            jnp.concatenate([other, held], axis=0),
        )
        span *= 2
    return held


def body(
    density,
    space_factor,
    diff_rate,
    loss_inverse,
    chain_yield,
    survival,
    gamma_yield,
    sky_weight,
    sky_blocks,
):
    groups = lax.axis_size("species")
    tiles = lax.axis_size("space")
    rows = NB // tiles

    field = density[0]
    bins = field.shape[0]
    depth = field.shape[3]
    rate = diff_rate[0][:, None, None, None]
    factor = rate * space_factor[None]
    halo = SUBSTEPS
    count = lax.axis_size("space")
    right_pairs = [(i, i + 1) for i in range(count - 1)]
    left_pairs = [(i + 1, i) for i in range(count - 1)]
    layers = field.shape[1]
    from_left = lax.ppermute(field[:, layers - halo:], "space", right_pairs)
    from_right = lax.ppermute(field[:, :halo], "space", left_pairs)
    factor_left = lax.ppermute(space_factor[layers - halo:], "space", right_pairs)
    factor_right = lax.ppermute(space_factor[:halo], "space", left_pairs)
    wide = jnp.concatenate([from_left, field, from_right], axis=1)
    wide_factor = rate * jnp.concatenate([factor_left, space_factor, factor_right], axis=0)[None]
    for step in range(SUBSTEPS):
        inner = wide[:, 1:-1]
        beside = wide[:, 2:] + wide[:, :-2] + cross_sum(inner)
        wide = inner + wide_factor[:, 1 + step:wide_factor.shape[1] - 1 - step] * (beside - 6.0 * inner)
    field = wide
    solved = jnp.dot(
        loss_inverse[0],
        field.reshape(bins, -1),
        precision=lax.Precision.HIGH,
        preferred_element_type=jnp.float32,
    ).reshape(field.shape)
    chain = chain_yield[0]
    own_part = survival[0][:, None, None, None] * solved

    own_columns = jnp.sum(own_part, axis=3).reshape(bins, -1)
    cols = own_columns.shape[1]
    extra = jnp.zeros((2, cols), jnp.float32).at[0, :bins].set(chain).at[1, :bins].set(gamma_yield[0])
    packed = jnp.concatenate([own_columns, extra], axis=0)
    me_g = lax.axis_index("species")
    everyone = packed[None]
    span = 1
    while span < groups:
        other = lax.ppermute(everyone, "species", [(i, i ^ span) for i in range(groups)])
        if span == 1:
            own_part, other = lax.optimization_barrier((own_part, other))
        low = (me_g & span) == 0
        everyone = jnp.where(
            low,
            jnp.concatenate([everyone, other], axis=0),
            jnp.concatenate([other, everyone], axis=0),
        )
        span *= 2
    sums = everyone[0, :bins]
    total = jnp.zeros((cols,), jnp.float32)
    for group in range(groups):
        if group > 0:
            sums = everyone[group, bins, :bins][:, None] * sums + everyone[group, :bins]
        weighted = jnp.dot(
            everyone[group, bins + 1, :bins], sums, precision=HIGH, preferred_element_type=jnp.float32
        )
        emission = lax.reduce_precision(weighted / (bins * depth), exponent_bits=8, mantissa_bits=7)
        total = total + emission
    contribution = jnp.einsum(
        "c,lcb->lb", total, sky_weight[0].astype(jnp.float32), precision=HIGH
    )
    lines, pixels = contribution.shape
    ids = jnp.zeros((1, pixels), jnp.float32).at[0, :lines].set(sky_blocks[0].astype(jnp.float32))
    payload = jnp.concatenate([contribution, ids], axis=0)
    base = bins // CHUNKS
    bounds = [0]
    for c in range(CHUNKS):
        bounds.append(bounds[-1] + base + 2 * c - (CHUNKS - 1))
    bounds[-1] = bins
    pieces = [own_part[bounds[c]:bounds[c + 1]] for c in range(CHUNKS)]
    scales = [chain[bounds[c]:bounds[c + 1]][:, None, None, None] for c in range(CHUNKS)]
    for wave in range(CHUNKS + groups - 2):
        for c in range(CHUNKS):
            s = wave - c
            if 0 <= s < groups - 1:
                arrived = lax.ppermute(pieces[c], "species", [(s, s + 1)])
                if s == 0 and c == CHUNKS - 1:
                    payload, arrived = lax.optimization_barrier((payload, arrived))
                pieces[c] = pieces[c] + scales[c] * arrived
    carried = jnp.concatenate(pieces, axis=0)
    gathered = gather_all(payload, "space")
    mine = lax.axis_index("space") * rows + jnp.arange(rows, dtype=jnp.int32)
    onehot = (
        gathered[:, lines, :lines].reshape(1, tiles * lines) == mine.astype(jnp.float32)[:, None]
    ).astype(jnp.float32)
    sky = jnp.dot(
        onehot,
        gathered[:, :lines].reshape(tiles * lines, pixels),
        precision=HIGH,
        preferred_element_type=jnp.float32,
    )

    return (carried[None], sky)


def solution(mesh):
    placed = (
        P("species", None, "space", None, None),
        P("space", None, None),
        P("species", None),
        P("species", None, None),
        P("species", None),
        P("species", None),
        P("species", None),
        P("space", None, None, None),
        P("space", None),
    )
    return jax.shard_map(
        body,
        mesh=mesh,
        in_specs=placed,
        out_specs=(P("species", None, "space", None, None), P("space", None)),
        check_vma=False,
    )
```

```python
import jax
import jax.numpy as jnp
from jax import lax
from jax.sharding import PartitionSpec as P

SUBSTEPS = 2
NB = 384
CHUNKS = 4
HIGH = lax.Precision.HIGHEST


def padded_2(cells, sides, width):
    for axis, dim in sides:
        count = lax.axis_size(axis)
        ends = count - 1
        head = lax.slice_in_dim(cells, 0, width, axis=dim)
        tail = lax.slice_in_dim(cells, cells.shape[dim] - width, cells.shape[dim], axis=dim)
        cells = jnp.concatenate(
            [
                lax.ppermute(tail, axis, [(i, (i + 1) % count) for i in range(ends)]),
                cells,
                lax.ppermute(head, axis, [((i + 1) % count, i) for i in range(ends)]),
            ],
            axis=dim,
        )
    return cells


def cross_sum(field):
    padded = jnp.pad(field, ((0, 0), (0, 0), (1, 1), (1, 1)))
    beside = padded[:, :, 2:, 1:-1] + padded[:, :, :-2, 1:-1]
    beside = beside + padded[:, :, 1:-1, 2:] + padded[:, :, 1:-1, :-2]
    return beside


def gather_all(block, axis):
    count = lax.axis_size(axis)
    if count & (count - 1):
        return lax.all_gather(block, axis)
    me = lax.axis_index(axis)
    held = block[None]
    span = 1
    while span < count:
        other = lax.ppermute(held, axis, [(i, i ^ span) for i in range(count)])
        low = (me & span) == 0
        held = jnp.where(
            low,
            jnp.concatenate([held, other], axis=0),
            jnp.concatenate([other, held], axis=0),
        )
        span *= 2
    return held


def body(
    density,
    space_factor,
    diff_rate,
    loss_inverse,
    chain_yield,
    survival,
    gamma_yield,
    sky_weight,
    sky_blocks,
):
    groups = lax.axis_size("species")
    tiles = lax.axis_size("space")
    rows = NB // tiles

    field = density[0]
    bins = field.shape[0]
    depth = field.shape[3]
    rate = diff_rate[0][:, None, None, None]
    factor = rate * space_factor[None]
    halo = SUBSTEPS
    count = lax.axis_size("space")
    right_pairs = [(i, i + 1) for i in range(count - 1)]
    left_pairs = [(i + 1, i) for i in range(count - 1)]
    layers = field.shape[1]
    from_left = lax.ppermute(field[:, layers - halo:], "space", right_pairs)
    from_right = lax.ppermute(field[:, :halo], "space", left_pairs)
    factor_left = lax.ppermute(space_factor[layers - halo:], "space", right_pairs)
    factor_right = lax.ppermute(space_factor[:halo], "space", left_pairs)
    wide = jnp.concatenate([from_left, field, from_right], axis=1)
    wide_factor = rate * jnp.concatenate([factor_left, space_factor, factor_right], axis=0)[None]
    for step in range(SUBSTEPS):
        inner = wide[:, 1:-1]
        beside = wide[:, 2:] + wide[:, :-2] + cross_sum(inner)
        wide = inner + wide_factor[:, 1 + step:wide_factor.shape[1] - 1 - step] * (beside - 6.0 * inner)
    field = wide
    solved = jnp.dot(
        loss_inverse[0],
        field.reshape(bins, -1),
        precision=lax.Precision.HIGH,
        preferred_element_type=jnp.float32,
    ).reshape(field.shape)
    chain = chain_yield[0]
    own_part = survival[0][:, None, None, None] * solved

    own_columns = jnp.sum(own_part, axis=3).reshape(bins, -1)
    cols = own_columns.shape[1]
    extra = jnp.zeros((2, cols), jnp.float32).at[0, :bins].set(chain).at[1, :bins].set(gamma_yield[0])
    packed = jnp.concatenate([own_columns, extra], axis=0)
    me_g = lax.axis_index("species")
    everyone = packed[None]
    span = 1
    while span < groups:
        other = lax.ppermute(everyone, "species", [(i, i ^ span) for i in range(groups)])
        if span == 1:
            own_part, other = lax.optimization_barrier((own_part, other))
        low = (me_g & span) == 0
        everyone = jnp.where(
            low,
            jnp.concatenate([everyone, other], axis=0),
            jnp.concatenate([other, everyone], axis=0),
        )
        span *= 2
    sums = everyone[0, :bins]
    total = jnp.zeros((cols,), jnp.float32)
    for group in range(groups):
        if group > 0:
            sums = everyone[group, bins, :bins][:, None] * sums + everyone[group, :bins]
        weighted = jnp.dot(
            everyone[group, bins + 1, :bins], sums, precision=HIGH, preferred_element_type=jnp.float32
        )
        emission = lax.reduce_precision(weighted / (bins * depth), exponent_bits=8, mantissa_bits=7)
        total = total + emission
    contribution = jnp.einsum(
        "c,lcb->lb", total, sky_weight[0].astype(jnp.float32), precision=HIGH
    )
    lines, pixels = contribution.shape
    ids = jnp.zeros((1, pixels), jnp.float32).at[0, :lines].set(sky_blocks[0].astype(jnp.float32))
    payload = jnp.concatenate([contribution, ids], axis=0)
    base = bins // CHUNKS
    bounds = [0]
    for step in (-2, -1, 1, 2):
        bounds.append(bounds[-1] + base + step)
    bounds[-1] = bins
    pieces = [own_part[bounds[c]:bounds[c + 1]] for c in range(CHUNKS)]
    scales = [chain[bounds[c]:bounds[c + 1]][:, None, None, None] for c in range(CHUNKS)]
    for wave in range(CHUNKS + groups - 2):
        for c in range(CHUNKS):
            s = wave - c
            if 0 <= s < groups - 1:
                arrived = lax.ppermute(pieces[c], "species", [(s, s + 1)])
                if s == 0 and c == CHUNKS - 1:
                    payload, arrived = lax.optimization_barrier((payload, arrived))
                pieces[c] = pieces[c] + scales[c] * arrived
    carried = jnp.concatenate(pieces, axis=0)
    gathered = gather_all(payload, "space")
    mine = lax.axis_index("space") * rows + jnp.arange(rows, dtype=jnp.int32)
    onehot = (
        gathered[:, lines, :lines].reshape(1, tiles * lines) == mine.astype(jnp.float32)[:, None]
    ).astype(jnp.float32)
    sky = jnp.dot(
        onehot,
        gathered[:, :lines].reshape(tiles * lines, pixels),
        precision=HIGH,
        preferred_element_type=jnp.float32,
    )

    return (carried[None], sky)


def solution(mesh):
    placed = (
        P("species", None, "space", None, None),
        P("space", None, None),
        P("species", None),
        P("species", None, None),
        P("species", None),
        P("species", None),
        P("species", None),
        P("space", None, None, None),
        P("space", None),
    )
    return jax.shard_map(
        body,
        mesh=mesh,
        in_specs=placed,
        out_specs=(P("species", None, "space", None, None), P("space", None)),
        check_vma=False,
    )
```

```python
import jax
import jax.numpy as jnp
from jax import lax
from jax.sharding import PartitionSpec as P

SUBSTEPS = 2
NB = 384
CHUNKS = 4
HIGH = lax.Precision.HIGHEST


def padded_2(cells, sides, width):
    for axis, dim in sides:
        count = lax.axis_size(axis)
        ends = count - 1
        head = lax.slice_in_dim(cells, 0, width, axis=dim)
        tail = lax.slice_in_dim(cells, cells.shape[dim] - width, cells.shape[dim], axis=dim)
        cells = jnp.concatenate(
            [
                lax.ppermute(tail, axis, [(i, (i + 1) % count) for i in range(ends)]),
                cells,
                lax.ppermute(head, axis, [((i + 1) % count, i) for i in range(ends)]),
            ],
            axis=dim,
        )
    return cells


def cross_sum(field):
    padded = jnp.pad(field, ((0, 0), (0, 0), (1, 1), (1, 1)))
    beside = padded[:, :, 2:, 1:-1] + padded[:, :, :-2, 1:-1]
    beside = beside + padded[:, :, 1:-1, 2:] + padded[:, :, 1:-1, :-2]
    return beside


def gather_all(block, axis):
    count = lax.axis_size(axis)
    if count & (count - 1):
        return lax.all_gather(block, axis)
    me = lax.axis_index(axis)
    held = block[None]
    span = 1
    while span < count:
        other = lax.ppermute(held, axis, [(i, i ^ span) for i in range(count)])
        low = (me & span) == 0
        held = jnp.where(
            low,
            jnp.concatenate([held, other], axis=0),
            jnp.concatenate([other, held], axis=0),
        )
        span *= 2
    return held


def body(
    density,
    space_factor,
    diff_rate,
    loss_inverse,
    chain_yield,
    survival,
    gamma_yield,
    sky_weight,
    sky_blocks,
):
    groups = lax.axis_size("species")
    tiles = lax.axis_size("space")
    rows = NB // tiles

    field = density[0]
    bins = field.shape[0]
    depth = field.shape[3]
    rate = diff_rate[0][:, None, None, None]
    factor = rate * space_factor[None]
    halo = SUBSTEPS
    count = lax.axis_size("space")
    right_pairs = [(i, i + 1) for i in range(count - 1)]
    left_pairs = [(i + 1, i) for i in range(count - 1)]
    layers = field.shape[1]
    from_left = lax.ppermute(field[:, layers - halo:], "space", right_pairs)
    from_right = lax.ppermute(field[:, :halo], "space", left_pairs)
    factor_left = lax.ppermute(space_factor[layers - halo:], "space", right_pairs)
    factor_right = lax.ppermute(space_factor[:halo], "space", left_pairs)
    wide = jnp.concatenate([from_left, field, from_right], axis=1)
    wide_factor = rate * jnp.concatenate([factor_left, space_factor, factor_right], axis=0)[None]
    for step in range(SUBSTEPS):
        inner = wide[:, 1:-1]
        beside = wide[:, 2:] + wide[:, :-2] + cross_sum(inner)
        wide = inner + wide_factor[:, 1 + step:wide_factor.shape[1] - 1 - step] * (beside - 6.0 * inner)
    field = wide
    solved = jnp.dot(
        loss_inverse[0],
        field.reshape(bins, -1),
        precision=lax.Precision.HIGH,
        preferred_element_type=jnp.float32,
    ).reshape(field.shape)
    chain = chain_yield[0]
    own_part = survival[0][:, None, None, None] * solved

    own_columns = jnp.sum(own_part, axis=3).reshape(bins, -1)
    cols = own_columns.shape[1]
    extra = jnp.zeros((2, cols), jnp.float32).at[0, :bins].set(chain).at[1, :bins].set(gamma_yield[0])
    packed = jnp.concatenate([own_columns, extra], axis=0)
    me_g = lax.axis_index("species")
    everyone = packed[None]
    span = 1
    while span < groups:
        other = lax.ppermute(everyone, "species", [(i, i ^ span) for i in range(groups)])
        if span == 1:
            own_part, other = lax.optimization_barrier((own_part, other))
        low = (me_g & span) == 0
        everyone = jnp.where(
            low,
            jnp.concatenate([everyone, other], axis=0),
            jnp.concatenate([other, everyone], axis=0),
        )
        span *= 2
    sums = everyone[0, :bins]
    total = jnp.zeros((cols,), jnp.float32)
    for group in range(groups):
        if group > 0:
            sums = everyone[group, bins, :bins][:, None] * sums + everyone[group, :bins]
        weighted = jnp.dot(
            everyone[group, bins + 1, :bins], sums, precision=HIGH, preferred_element_type=jnp.float32
        )
        emission = lax.reduce_precision(weighted / (bins * depth), exponent_bits=8, mantissa_bits=7)
        total = total + emission
    contribution = jnp.einsum(
        "c,lcb->lb", total, sky_weight[0].astype(jnp.float32), precision=HIGH
    )
    lines, pixels = contribution.shape
    ids = jnp.zeros((1, pixels), jnp.float32).at[0, :lines].set(sky_blocks[0].astype(jnp.float32))
    payload = jnp.concatenate([contribution, ids], axis=0)
    base = bins // CHUNKS
    bounds = [0]
    for step in (-3, 0, 1, 2):
        bounds.append(bounds[-1] + base + step)
    bounds[-1] = bins
    pieces = [own_part[bounds[c]:bounds[c + 1]] for c in range(CHUNKS)]
    scales = [chain[bounds[c]:bounds[c + 1]][:, None, None, None] for c in range(CHUNKS)]
    for wave in range(CHUNKS + groups - 2):
        for c in range(CHUNKS):
            s = wave - c
            if 0 <= s < groups - 1:
                arrived = lax.ppermute(pieces[c], "species", [(s, s + 1)])
                if s == 0 and c == CHUNKS - 1:
                    payload, arrived = lax.optimization_barrier((payload, arrived))
                pieces[c] = pieces[c] + scales[c] * arrived
    carried = jnp.concatenate(pieces, axis=0)
    gathered = gather_all(payload, "space")
    mine = lax.axis_index("space") * rows + jnp.arange(rows, dtype=jnp.int32)
    onehot = (
        gathered[:, lines, :lines].reshape(1, tiles * lines) == mine.astype(jnp.float32)[:, None]
    ).astype(jnp.float32)
    sky = jnp.dot(
        onehot,
        gathered[:, :lines].reshape(tiles * lines, pixels),
        precision=HIGH,
        preferred_element_type=jnp.float32,
    )

    return (carried[None], sky)


def solution(mesh):
    placed = (
        P("species", None, "space", None, None),
        P("space", None, None),
        P("species", None),
        P("species", None, None),
        P("species", None),
        P("species", None),
        P("species", None),
        P("space", None, None, None),
        P("space", None),
    )
    return jax.shard_map(
        body,
        mesh=mesh,
        in_specs=placed,
        out_specs=(P("species", None, "space", None, None), P("space", None)),
        check_vma=False,
    )
```
